128 devices in a mesh: rows: 32 (over y, x, z_lo), cols: 4 (over z_hi, core).
Axes of the slice: x: 4, y: 4, z: 4 (z_hi: 2, z_lo: 2; z = z_hi * 2 + z_lo), core: 2. Of those that a mesh axis runs over, the one named last changes fastest.
Arguments:
- block_input: bfloat16 [2, 128, 128, 1536], P(None, 'rows', 'cols'), may hold values from -6 to 6
- token_grads: bfloat16 [2, 4096, 6144], P(None, ('rows', 'cols')), may hold values from -6 to 6
- conv_kernel: float32 [7, 7, 1536], replicated, may hold values from -0.875 to 0.875
- layer_norm_gain: float32 [1536], replicated, may hold values from 0.25 to 1.75
- w_in: bfloat16 [1536, 3072], P('rows', 'cols'), may hold values from -0.15625 to 0.15625
- w_out: bfloat16 [3072, 1536], P('cols', 'rows'), may hold values from -0.109375 to 0.109375
- layer_scale: float32 [1536], replicated, may hold values from 0.25 to 1.75
Outputs:
- input_grad: bfloat16 [2, 128, 128, 1536], P(None, 'rows', 'cols')
- grad_w1: float32 [1536, 3072], P('rows', 'cols')
- grad_w2: float32 [3072, 1536], P('cols', 'rows')
- grad_kernel: float32 [7, 7, 1536], replicated
The draws below stay inside these ranges and needn't reach their ends.
All inputs are finite; a program needn't handle non-finite values.
Results may differ from the reference program's by a relative error of at most 0.0062.
Values may be sent and summed in bfloat16 or wider, within the bound.
No kernel may reach another device: no remote copies, remote signals or barrier semaphores. Data moves between devices by JAX's collectives and lax.ppermute only.
A program may use at most 128 MiB of HBM per device.

```python
import jax
import jax.numpy as jnp
from jax import lax

CHANNEL_COUNT = 1536
F = 3072
KS = 7
IMAGES = 2
H = 128
W = 128
MTOK = 4096


def level_of(stream_key, dims, cuts, least, top_value):
    level, own = 1.0, jax.random.fold_in(stream_key, 6)
    for position, blocks in cuts:
        heights = jnp.exp(jax.random.uniform(jax.random.fold_in(own, position), (blocks,), jnp.float32, least / len(cuts), top_value / len(cuts)))
        level = level * jnp.repeat(heights, dims[position] // blocks).reshape([-1 if axis == position else 1 for axis in range(len(dims))])
    return level


def scatter_about(key, shape, scale, bound, split=(), dtype=jnp.bfloat16):
    drawn = scale * jax.random.normal(key, shape, jnp.float32)
    if split:
        drawn = drawn * level_of(key, shape, split, -0.22, 0.18)
    return jnp.clip(drawn, -bound, bound).astype(dtype)


def setup_inputs(seed: int = 0) -> dict:
    key_list = jax.random.split(jax.random.key(seed), 8)
    return {
        "block_input": scatter_about(key_list[0], (IMAGES, H, W, CHANNEL_COUNT), 1.0, 6.0, ((1, 32), (2, 4))),
        "token_grads": scatter_about(key_list[1], (IMAGES, MTOK, 4 * CHANNEL_COUNT), 1.0, 6.0, ((1, 128),)),
        "conv_kernel": scatter_about(key_list[2], (KS, KS, CHANNEL_COUNT), (KS * KS) ** -0.5, 0.875, (), jnp.float32),
        "layer_norm_gain": jnp.clip(1.0 + 0.15 * jax.random.normal(key_list[3], (CHANNEL_COUNT,), jnp.float32), 0.25, 1.75),
        "w_in": scatter_about(key_list[4], (CHANNEL_COUNT, F), CHANNEL_COUNT ** -0.5, 0.15625, ((0, 32), (1, 4))),
        "w_out": scatter_about(key_list[5], (F, CHANNEL_COUNT), F ** -0.5, 0.109375, ((0, 4), (1, 32))),
        "layer_scale": jnp.clip(1.0 + 0.15 * jax.random.normal(key_list[6], (CHANNEL_COUNT,), jnp.float32), 0.25, 1.75),
    }


def reference(block_input, token_grads, conv_kernel, layer_norm_gain, w_in, w_out, layer_scale):
    kernel_reach = KS // 2
    out_grad = token_grads.reshape(IMAGES, H // 2, W // 2, 2, 2, CHANNEL_COUNT)
    out_grad = out_grad.transpose(0, 1, 3, 2, 4, 5).reshape(IMAGES, H, W, CHANNEL_COUNT)
    input_f32 = block_input.astype(jnp.float32)
    padded = jnp.pad(input_f32, ((0, 0), (kernel_reach, kernel_reach), (kernel_reach, kernel_reach), (0, 0)))
    conv_out = jnp.zeros((IMAGES, H, W, CHANNEL_COUNT), jnp.float32)
    for r in range(KS):
        for s in range(KS):
            conv_out = conv_out + conv_kernel[r, s] * padded[:, r:r + H, s:s + W]
    mean_val = lax.optimization_barrier(jnp.mean(conv_out, axis=-1, keepdims=True))
    centered_input = conv_out - mean_val
    var_val = lax.optimization_barrier(jnp.mean(centered_input * centered_input, axis=-1, keepdims=True))
    inverse_deviation = lax.rsqrt(var_val + 1e-06)
    standardized_input = centered_input * inverse_deviation
    norm_output = (standardized_input * layer_norm_gain).astype(jnp.bfloat16).reshape(-1, CHANNEL_COUNT)
    pre = jnp.dot(norm_output, w_in, preferred_element_type=jnp.float32)
    cdf = 0.5 * (1.0 + lax.erf(pre * 0.7071067811865476))
    hidden = (pre * cdf).astype(jnp.bfloat16)
    branch_grad = (out_grad.astype(jnp.float32) * layer_scale).astype(jnp.bfloat16).reshape(-1, CHANNEL_COUNT)
    back_hidden = lax.dot_general(branch_grad, w_out, (((1,), (1,)), ((), ())), preferred_element_type=jnp.float32)
    density = jnp.exp(-0.5 * pre * pre) * 0.3989422804014327
    hidden_grad = (back_hidden * (cdf + pre * density)).astype(jnp.bfloat16)
    scale = 1.0 / float(IMAGES * H * W) ** 0.5
    grad_w2 = lax.dot_general(hidden, branch_grad, (((0,), (0,)), ((), ())), preferred_element_type=jnp.float32) * scale
    grad_w1 = lax.dot_general(norm_output, hidden_grad, (((0,), (0,)), ((), ())), preferred_element_type=jnp.float32) * scale
    normed_grad = lax.dot_general(hidden_grad, w_in, (((1,), (1,)), ((), ())), preferred_element_type=jnp.float32)
    gain_applied = normed_grad.reshape(IMAGES, H, W, CHANNEL_COUNT) * layer_norm_gain
    convolution_gradient = inverse_deviation * (gain_applied - lax.optimization_barrier(jnp.mean(gain_applied, axis=-1, keepdims=True)) - standardized_input * lax.optimization_barrier(jnp.mean(gain_applied * standardized_input, axis=-1, keepdims=True)))
    kernel_rows = []
    for r in range(KS):
        row_terms = []
        for s in range(KS):
            row_terms.append(lax.optimization_barrier(jnp.sum(convolution_gradient * padded[:, r:r + H, s:s + W], axis=(0, 1, 2))))
        kernel_rows.append(jnp.stack(row_terms))
    grad_kernel = jnp.stack(kernel_rows) * scale
    grad_pad = jnp.pad(convolution_gradient, ((0, 0), (kernel_reach, kernel_reach), (kernel_reach, kernel_reach), (0, 0)))
    total = out_grad.astype(jnp.float32)
    for r in range(KS):
        for s in range(KS):
            total = total + conv_kernel[r, s] * grad_pad[:, 2 * kernel_reach - r:2 * kernel_reach - r + H, 2 * kernel_reach - s:2 * kernel_reach - s + W]
    input_grad = total.astype(jnp.bfloat16)
    return (input_grad, grad_w1, grad_w2, grad_kernel)
```

```python
import jax
import jax.numpy as jnp
from jax import lax
from jax.sharding import PartitionSpec as P


def with_halo(value, sides, width):
    for axis, dim in sides:
        peers, length = (lax.axis_size(axis), value.shape[dim])
        up = [(i, (i + 1) % peers) for i in range(peers - 1)]
        down = [(j, i) for i, j in up]
        last = lax.slice_in_dim(value, length - width, length, axis=dim)
        first = lax.slice_in_dim(value, 0, width, axis=dim)
        before = lax.ppermute(last, axis, up)
        after = lax.ppermute(first, axis, down)
        value = jnp.concatenate([before, value, after], axis=dim)
    return value


def swap_with(value, axis, bit):
    peers = lax.axis_size(axis)
    return lax.ppermute(value, axis, [(i, i ^ (1 << bit)) for i in range(peers)])


def gather_rows(value, axis, order):
    me = lax.axis_index(axis)
    for bit in order:
        other = swap_with(value, axis, bit)
        b = (me >> bit) & 1
        both = jnp.concatenate([value, other, value], axis=0)
        value = lax.dynamic_slice_in_dim(both, b * value.shape[0], 2 * value.shape[0], axis=0)
    n = len(order)
    block = value.shape[0] >> n
    rest = value.shape[1:]
    value = value.reshape((2,) * n + (block,) + rest)
    perm = [n - 1 - order.index(k) for k in reversed(range(n))]
    value = value.transpose(perm + list(range(n, value.ndim)))
    return value.reshape((block << n,) + rest)


def scatter_rows(value, axis, order):
    me = lax.axis_index(axis)
    n = len(order)
    block = value.shape[0] >> n
    rest = value.shape[1:]
    value = value.reshape((2,) * n + (block,) + rest)
    perm = [n - 1 - order[j] for j in range(n)]
    value = value.transpose(perm + list(range(n, value.ndim))).reshape((block << n,) + rest)
    for bit in order:
        half = value.shape[0] // 2
        b = (me >> bit) & 1
        keep = lax.dynamic_slice_in_dim(value, b * half, half, axis=0)
        send = lax.dynamic_slice_in_dim(value, (1 - b) * half, half, axis=0)
        value = keep + swap_with(send, axis, bit)
    return value


def local(block_input, token_grads, conv_kernel, layer_norm_gain, w_in, w_out, layer_scale):
    images, tile_rows, tile_cols, channel_total = block_input.shape
    kernel_size = conv_kernel.shape[0]
    kernel_reach = kernel_size // 2
    n_rows = lax.axis_size("rows")
    n_cols = lax.axis_size("cols")
    row_bits = n_rows.bit_length() - 1
    col_bits = n_cols.bit_length() - 1
    run_count = tile_rows // 2
    half_cols = tile_cols // 2
    col_index = lax.axis_index("cols")

    w_in_cols = gather_rows(w_in, "rows", (4, 2, 3, 1, 0))
    w_out_cols_t = gather_rows(w_out.T, "rows", (4, 2, 3, 0, 1))

    tokens = token_grads.reshape(images, 2, half_cols, 4 * channel_total)
    first_half = col_index // 2
    send_a = lax.dynamic_index_in_dim(tokens, first_half, 1, keepdims=False)
    send_b = lax.dynamic_index_in_dim(tokens, 1 - first_half, 1, keepdims=False)
    got_a = lax.ppermute(send_a, "cols", [(s, 2 * (s % 2) + s // 2) for s in range(n_cols)])
    got_b = lax.ppermute(send_b, "cols", [(s, 2 * (s % 2) + 1 - s // 2) for s in range(n_cols)])
    merged = lax.dynamic_slice_in_dim(
        jnp.stack([got_a, got_b, got_a], axis=1), col_index % 2, 2, axis=1
    )
    out_grad = merged.reshape(images, run_count, half_cols, 2, 2, channel_total)
    out_grad = out_grad.transpose(0, 1, 3, 2, 4, 5).reshape(
        images, tile_rows, tile_cols, channel_total
    )
    padded = with_halo(block_input, (("rows", 1), ("cols", 2)), kernel_reach)
    padded = padded.astype(jnp.float32)
    conv_out = jnp.zeros((images, tile_rows, tile_cols, channel_total), jnp.float32)
    for r in range(kernel_size):
        for s in range(kernel_size):
            conv_out = (
                conv_out + conv_kernel[r, s] * padded[:, r : r + tile_rows, s : s + tile_cols]
            )
    mean_val = jnp.mean(conv_out, axis=-1, keepdims=True)
    centered_input = conv_out - mean_val
    var_val = jnp.mean(centered_input * centered_input, axis=-1, keepdims=True)
    inverse_deviation = lax.rsqrt(var_val + 1e-06)
    standardized_input = centered_input * inverse_deviation
    pixel_total = images * tile_rows * tile_cols
    norm_output = (
        (standardized_input * layer_norm_gain)
        .astype(jnp.bfloat16)
        .reshape(pixel_total, channel_total)
    )
    branch_grad = (
        (out_grad.astype(jnp.float32) * layer_scale)
        .astype(jnp.bfloat16)
        .reshape(pixel_total, channel_total)
    )
    branch_all = lax.all_gather(branch_grad, "cols", axis=0, tiled=True)
    normed_all = lax.all_gather(norm_output, "cols", axis=0, tiled=True)
    pre = jnp.dot(normed_all, w_in_cols, preferred_element_type=jnp.float32)
    cdf = 0.5 * (1.0 + lax.erf(pre * 0.7071067811865476))
    hidden = (pre * cdf).astype(jnp.bfloat16)
    back_hidden = jnp.dot(branch_all, w_out_cols_t, preferred_element_type=jnp.float32)
    density = jnp.exp(-0.5 * pre * pre) * 0.3989422804014327
    hidden_grad = (back_hidden * (cdf + pre * density)).astype(jnp.bfloat16)
    scale = 1.0 / float(images * tile_rows * tile_cols * n_rows * n_cols) ** 0.5
    out_terms_t = lax.dot_general(
        branch_all, hidden, (((0,), (0,)), ((), ())), preferred_element_type=jnp.float32
    )
    in_terms = lax.dot_general(
        normed_all, hidden_grad, (((0,), (0,)), ((), ())), preferred_element_type=jnp.float32
    )
    grad_w1 = scatter_rows(in_terms, "rows", (0, 1, 3, 2, 4)) * scale
    grad_w2 = (scatter_rows(out_terms_t, "rows", (1, 0, 3, 2, 4)) * scale).T
    normed_grad = lax.psum_scatter(
        lax.dot_general(
            hidden_grad, w_in_cols, (((1,), (1,)), ((), ())), preferred_element_type=jnp.float32
        ),
        "cols",
        scatter_dimension=0,
        tiled=True,
    )
    gain_applied = (
        normed_grad.reshape(images, tile_rows, tile_cols, channel_total) * layer_norm_gain
    )
    convolution_gradient = inverse_deviation * (
        gain_applied
        - jnp.mean(gain_applied, axis=-1, keepdims=True)
        - standardized_input * jnp.mean(gain_applied * standardized_input, axis=-1, keepdims=True)
    )
    kernel_rows = []
    for r in range(kernel_size):
        row_terms = []
        for s in range(kernel_size):
            row_terms.append(
                jnp.sum(
                    convolution_gradient * padded[:, r : r + tile_rows, s : s + tile_cols],
                    axis=(0, 1, 2),
                )
            )
        kernel_rows.append(jnp.stack(row_terms))
    grad_kernel = jnp.stack(kernel_rows)
    for bit in range(col_bits):
        grad_kernel = grad_kernel + swap_with(grad_kernel, "cols", bit)
    for bit in (0, 1, 3, 2, 4)[:row_bits]:
        grad_kernel = grad_kernel + swap_with(grad_kernel, "rows", bit)
    grad_kernel = grad_kernel * scale
    grad_pad = with_halo(convolution_gradient, (("rows", 1), ("cols", 2)), kernel_reach)
    total = out_grad.astype(jnp.float32)
    for r in range(kernel_size):
        for s in range(kernel_size):
            row_from = 2 * kernel_reach - r
            col_from = 2 * kernel_reach - s
            total = (
                total
                + conv_kernel[r, s]
                * grad_pad[:, row_from : row_from + tile_rows, col_from : col_from + tile_cols]
            )
    input_grad = total.astype(jnp.bfloat16)
    return (input_grad, grad_w1, grad_w2, grad_kernel)


def solution(mesh):
    return jax.shard_map(
        local,
        mesh=mesh,
        in_specs=(
            P(None, "rows", "cols", None),
            P(None, ("rows", "cols"), None),
            P(),
            P(),
            P("rows", "cols"),
            P("cols", "rows"),
            P(),
        ),
        out_specs=(P(None, "rows", "cols", None), P("rows", "cols"), P("cols", "rows"), P()),
        check_vma=False,
    )
```

```python
import jax
import jax.numpy as jnp
from jax import lax
from jax.sharding import PartitionSpec as P


def with_halo(value, sides, width):
    for axis, dim in sides:
        peers, length = (lax.axis_size(axis), value.shape[dim])
        up = [(i, (i + 1) % peers) for i in range(peers - 1)]
        down = [(j, i) for i, j in up]
        last = lax.slice_in_dim(value, length - width, length, axis=dim)
        first = lax.slice_in_dim(value, 0, width, axis=dim)
        before = lax.ppermute(last, axis, up)
        after = lax.ppermute(first, axis, down)
        value = jnp.concatenate([before, value, after], axis=dim)
    return value


def swap_with(value, axis, bit):
    peers = lax.axis_size(axis)
    return lax.ppermute(value, axis, [(i, i ^ (1 << bit)) for i in range(peers)])


def gather_rows(value, axis, order):
    me = lax.axis_index(axis)
    for bit in order:
        other = swap_with(value, axis, bit)
        b = (me >> bit) & 1
        both = jnp.concatenate([value, other, value], axis=0)
        value = lax.dynamic_slice_in_dim(both, b * value.shape[0], 2 * value.shape[0], axis=0)
    n = len(order)
    block = value.shape[0] >> n
    rest = value.shape[1:]
    value = value.reshape((2,) * n + (block,) + rest)
    perm = [n - 1 - order.index(k) for k in reversed(range(n))]
    value = value.transpose(perm + list(range(n, value.ndim)))
    return value.reshape((block << n,) + rest)


def scatter_rows(value, axis, order):
    me = lax.axis_index(axis)
    n = len(order)
    block = value.shape[0] >> n
    rest = value.shape[1:]
    value = value.reshape((2,) * n + (block,) + rest)
    perm = [n - 1 - order[j] for j in range(n)]
    value = value.transpose(perm + list(range(n, value.ndim))).reshape((block << n,) + rest)
    for bit in order:
        half = value.shape[0] // 2
        b = (me >> bit) & 1
        keep = lax.dynamic_slice_in_dim(value, b * half, half, axis=0)
        send = lax.dynamic_slice_in_dim(value, (1 - b) * half, half, axis=0)
        value = keep + swap_with(send, axis, bit)
    return value


def local(block_input, token_grads, conv_kernel, layer_norm_gain, w_in, w_out, layer_scale):
    images, tile_rows, tile_cols, channel_total = block_input.shape
    kernel_size = conv_kernel.shape[0]
    kernel_reach = kernel_size // 2
    n_rows = lax.axis_size("rows")
    n_cols = lax.axis_size("cols")
    row_bits = n_rows.bit_length() - 1
    col_bits = n_cols.bit_length() - 1
    run_count = tile_rows // 2
    half_cols = tile_cols // 2
    col_index = lax.axis_index("cols")

    w_in_cols = gather_rows(w_in, "rows", (4, 2, 3, 1, 0))
    w_out_cols_t = gather_rows(w_out.T, "rows", (4, 2, 3, 0, 1))

    tokens = token_grads.reshape(images, 2, half_cols, 4 * channel_total)
    first_half = col_index // 2
    send_a = lax.dynamic_index_in_dim(tokens, first_half, 1, keepdims=False)
    send_b = lax.dynamic_index_in_dim(tokens, 1 - first_half, 1, keepdims=False)
    got_a = lax.ppermute(send_a, "cols", [(s, 2 * (s % 2) + s // 2) for s in range(n_cols)])
    got_b = lax.ppermute(send_b, "cols", [(s, 2 * (s % 2) + 1 - s // 2) for s in range(n_cols)])
    merged = lax.dynamic_slice_in_dim(
        jnp.stack([got_a, got_b, got_a], axis=1), col_index % 2, 2, axis=1
    )
    out_grad = merged.reshape(images, run_count, half_cols, 2, 2, channel_total)
    out_grad = out_grad.transpose(0, 1, 3, 2, 4, 5).reshape(
        images, tile_rows, tile_cols, channel_total
    )
    lane = 128
    groups = channel_total // lane

    def to_tiles(x):
        x = x.reshape(images, tile_rows, tile_cols, groups, lane).transpose(1, 2, 0, 3, 4)
        return x.reshape(tile_rows, tile_cols, images * groups, lane)

    def from_tiles(t):
        t = t.reshape(tile_rows, tile_cols, images, groups, lane).transpose(2, 0, 1, 3, 4)
        return t.reshape(images, tile_rows, tile_cols, channel_total)

    taps = jnp.tile(
        conv_kernel.reshape(kernel_size, kernel_size, 1, groups, lane), (1, 1, images, 1, 1)
    ).reshape(kernel_size, kernel_size, images * groups, lane)
    padded = with_halo(to_tiles(block_input), (("rows", 0), ("cols", 1)), kernel_reach)
    conv_t = jnp.zeros((tile_rows, tile_cols, images * groups, lane), jnp.float32)
    for r in range(kernel_size):
        for s in range(kernel_size):
            conv_t = conv_t + taps[r, s] * padded[r : r + tile_rows, s : s + tile_cols].astype(
                jnp.float32
            )
    conv_out = from_tiles(conv_t)
    mean_val = jnp.mean(conv_out, axis=-1, keepdims=True)
    centered_input = conv_out - mean_val
    var_val = jnp.mean(centered_input * centered_input, axis=-1, keepdims=True)
    inverse_deviation = lax.rsqrt(var_val + 1e-06)
    standardized_input = centered_input * inverse_deviation
    pixel_total = images * tile_rows * tile_cols
    norm_output = (
        (standardized_input * layer_norm_gain)
        .astype(jnp.bfloat16)
        .reshape(pixel_total, channel_total)
    )
    branch_grad = (
        (out_grad.astype(jnp.float32) * layer_scale)
        .astype(jnp.bfloat16)
        .reshape(pixel_total, channel_total)
    )
    branch_all = lax.all_gather(branch_grad, "cols", axis=0, tiled=True)
    normed_all = lax.all_gather(norm_output, "cols", axis=0, tiled=True)
    pre = jnp.dot(normed_all, w_in_cols, preferred_element_type=jnp.float32)
    cdf = 0.5 * (1.0 + lax.erf(pre * 0.7071067811865476))
    hidden = (pre * cdf).astype(jnp.bfloat16)
    back_hidden = jnp.dot(branch_all, w_out_cols_t, preferred_element_type=jnp.float32)
    density = jnp.exp(-0.5 * pre * pre) * 0.3989422804014327
    hidden_grad = (back_hidden * (cdf + pre * density)).astype(jnp.bfloat16)
    scale = 1.0 / float(images * tile_rows * tile_cols * n_rows * n_cols) ** 0.5
    out_terms_t = lax.dot_general(
        branch_all, hidden, (((0,), (0,)), ((), ())), preferred_element_type=jnp.float32
    )
    in_terms = lax.dot_general(
        normed_all, hidden_grad, (((0,), (0,)), ((), ())), preferred_element_type=jnp.float32
    )
    grad_w1 = scatter_rows(in_terms, "rows", (0, 1, 3, 2, 4)) * scale
    grad_w2 = (scatter_rows(out_terms_t, "rows", (1, 0, 3, 2, 4)) * scale).T
    normed_grad = scatter_rows(
        lax.dot_general(
            hidden_grad, w_in_cols, (((1,), (1,)), ((), ())), preferred_element_type=jnp.float32
        ),
        "cols",
        (0, 1)[:col_bits],
    )
    gain_applied = (
        normed_grad.reshape(images, tile_rows, tile_cols, channel_total) * layer_norm_gain
    )
    convolution_gradient = inverse_deviation * (
        gain_applied
        - jnp.mean(gain_applied, axis=-1, keepdims=True)
        - standardized_input * jnp.mean(gain_applied * standardized_input, axis=-1, keepdims=True)
    )
    grad_t = to_tiles(convolution_gradient)
    kernel_rows = []
    for r in range(kernel_size):
        row_terms = []
        for s in range(kernel_size):
            term = jnp.sum(
                grad_t * padded[r : r + tile_rows, s : s + tile_cols].astype(jnp.float32),
                axis=(0, 1),
            )
            row_terms.append(term.reshape(images, channel_total).sum(axis=0))
        kernel_rows.append(jnp.stack(row_terms))
    grad_kernel = jnp.stack(kernel_rows)
    for bit in range(col_bits):
        grad_kernel = grad_kernel + swap_with(grad_kernel, "cols", bit)
    for bit in (0, 1, 3, 2, 4)[:row_bits]:
        grad_kernel = grad_kernel + swap_with(grad_kernel, "rows", bit)
    grad_kernel = grad_kernel * scale
    grad_pad = with_halo(grad_t, (("rows", 0), ("cols", 1)), kernel_reach)
    total = to_tiles(out_grad).astype(jnp.float32)
    for r in range(kernel_size):
        for s in range(kernel_size):
            row_from = 2 * kernel_reach - r
            col_from = 2 * kernel_reach - s
            total = (
                total
                + taps[r, s]
                * grad_pad[row_from : row_from + tile_rows, col_from : col_from + tile_cols]
            )
    total = from_tiles(total)
    input_grad = total.astype(jnp.bfloat16)
    return (input_grad, grad_w1, grad_w2, grad_kernel)


def solution(mesh):
    return jax.shard_map(
        local,
        mesh=mesh,
        in_specs=(
            P(None, "rows", "cols", None),
            P(None, ("rows", "cols"), None),
            P(),
            P(),
            P("rows", "cols"),
            P("cols", "rows"),
            P(),
        ),
        out_specs=(P(None, "rows", "cols", None), P("rows", "cols"), P("cols", "rows"), P()),
        check_vma=False,
    )
```

```python
import jax
import jax.numpy as jnp
from jax import lax
from jax.sharding import PartitionSpec as P


def with_halo(value, sides, width):
    for axis, dim in sides:
        peers, length = (lax.axis_size(axis), value.shape[dim])
        up = [(i, (i + 1) % peers) for i in range(peers - 1)]
        down = [(j, i) for i, j in up]
        last = lax.slice_in_dim(value, length - width, length, axis=dim)
        first = lax.slice_in_dim(value, 0, width, axis=dim)
        before = lax.ppermute(last, axis, up)
        after = lax.ppermute(first, axis, down)
        value = jnp.concatenate([before, value, after], axis=dim)
    return value


def swap_with(value, axis, bit):
    peers = lax.axis_size(axis)
    return lax.ppermute(value, axis, [(i, i ^ (1 << bit)) for i in range(peers)])


def gather_rows(value, axis, order):
    me = lax.axis_index(axis)
    for bit in order:
        other = swap_with(value, axis, bit)
        b = (me >> bit) & 1
        both = jnp.concatenate([value, other, value], axis=0)
        value = lax.dynamic_slice_in_dim(both, b * value.shape[0], 2 * value.shape[0], axis=0)
    n = len(order)
    block = value.shape[0] >> n
    rest = value.shape[1:]
    value = value.reshape((2,) * n + (block,) + rest)
    perm = [n - 1 - order.index(k) for k in reversed(range(n))]
    value = value.transpose(perm + list(range(n, value.ndim)))
    return value.reshape((block << n,) + rest)


def scatter_rows(value, axis, order):
    me = lax.axis_index(axis)
    n = len(order)
    block = value.shape[0] >> n
    rest = value.shape[1:]
    value = value.reshape((2,) * n + (block,) + rest)
    perm = [n - 1 - order[j] for j in range(n)]
    value = value.transpose(perm + list(range(n, value.ndim))).reshape((block << n,) + rest)
    for bit in order:
        half = value.shape[0] // 2
        b = (me >> bit) & 1
        keep = lax.dynamic_slice_in_dim(value, b * half, half, axis=0)
        send = lax.dynamic_slice_in_dim(value, (1 - b) * half, half, axis=0)
        value = keep + swap_with(send, axis, bit)
    return value


GATHER_ORDERS = ((4, 2, 3, 1, 0), (2, 4, 0, 3, 1), (4, 2, 1, 0, 3))
SCATTER_ORDERS = ((0, 1, 3, 2, 4), (1, 3, 0, 4, 2), (3, 0, 1, 2, 4))


def scatter_split(value):
    third = value.shape[1] // 3
    return jnp.concatenate(
        [
            scatter_rows(value[:, i * third : (i + 1) * third], "rows", order)
            for i, order in enumerate(SCATTER_ORDERS)
        ],
        axis=1,
    )


def local(block_input, token_grads, conv_kernel, layer_norm_gain, w_in, w_out, layer_scale):
    images, tile_rows, tile_cols, channel_total = block_input.shape
    kernel_size = conv_kernel.shape[0]
    kernel_reach = kernel_size // 2
    n_rows = lax.axis_size("rows")
    n_cols = lax.axis_size("cols")
    row_bits = n_rows.bit_length() - 1
    col_bits = n_cols.bit_length() - 1
    run_count = tile_rows // 2
    half_cols = tile_cols // 2
    col_index = lax.axis_index("cols")

    hidden_cols = w_in.shape[1]
    both_weights = jnp.concatenate([w_in, w_out.T], axis=1)
    third = both_weights.shape[1] // 3
    gathered = jnp.concatenate(
        [
            gather_rows(both_weights[:, i * third : (i + 1) * third], "rows", order)
            for i, order in enumerate(GATHER_ORDERS)
        ],
        axis=1,
    )
    w_in_cols = gathered[:, :hidden_cols]
    w_out_cols_t = gathered[:, hidden_cols:]

    tokens = token_grads.reshape(images, 2, half_cols, 4 * channel_total)
    first_half = col_index // 2
    send_a = lax.dynamic_index_in_dim(tokens, first_half, 1, keepdims=False)
    send_b = lax.dynamic_index_in_dim(tokens, 1 - first_half, 1, keepdims=False)
    got_a = lax.ppermute(send_a, "cols", [(s, 2 * (s % 2) + s // 2) for s in range(n_cols)])
    got_b = lax.ppermute(send_b, "cols", [(s, 2 * (s % 2) + 1 - s // 2) for s in range(n_cols)])
    merged = lax.dynamic_slice_in_dim(
        jnp.stack([got_a, got_b, got_a], axis=1), col_index % 2, 2, axis=1
    )
    out_grad = merged.reshape(images, run_count, half_cols, 2, 2, channel_total)
    out_grad = out_grad.transpose(0, 1, 3, 2, 4, 5).reshape(
        images, tile_rows, tile_cols, channel_total
    )
    pixel_total = images * tile_rows * tile_cols
    branch_grad = (
        (out_grad.astype(jnp.float32) * layer_scale)
        .astype(jnp.bfloat16)
        .reshape(pixel_total, channel_total)
    )
    branch_all = gather_rows(branch_grad, "cols", (1, 0)[:col_bits])
    lane = 128
    groups = channel_total // lane

    def to_tiles(x):
        x = x.reshape(images, tile_rows, tile_cols, groups, lane).transpose(1, 2, 0, 3, 4)
        return x.reshape(tile_rows, tile_cols, images * groups, lane)

    def from_tiles(t):
        t = t.reshape(tile_rows, tile_cols, images, groups, lane).transpose(2, 0, 1, 3, 4)
        return t.reshape(images, tile_rows, tile_cols, channel_total)

    taps = jnp.tile(
        conv_kernel.reshape(kernel_size, kernel_size, 1, groups, lane), (1, 1, images, 1, 1)
    ).reshape(kernel_size, kernel_size, images * groups, lane)
    padded = with_halo(to_tiles(block_input), (("rows", 0), ("cols", 1)), kernel_reach)
    w_in_cols, w_out_cols_t, branch_all, padded = lax.optimization_barrier(
        (w_in_cols, w_out_cols_t, branch_all, padded)
    )
    conv_t = jnp.zeros((tile_rows, tile_cols, images * groups, lane), jnp.float32)
    for r in range(kernel_size):
        for s in range(kernel_size):
            conv_t = conv_t + taps[r, s] * padded[r : r + tile_rows, s : s + tile_cols].astype(
                jnp.float32
            )
    conv_out = from_tiles(conv_t)
    mean_val = jnp.mean(conv_out, axis=-1, keepdims=True)
    centered_input = conv_out - mean_val
    var_val = jnp.mean(centered_input * centered_input, axis=-1, keepdims=True)
    inverse_deviation = lax.rsqrt(var_val + 1e-06)
    standardized_input = centered_input * inverse_deviation
    norm_output = (
        (standardized_input * layer_norm_gain)
        .astype(jnp.bfloat16)
        .reshape(pixel_total, channel_total)
    )
    normed_all = lax.all_gather(norm_output, "cols", axis=0, tiled=True)
    pre = jnp.dot(normed_all, w_in_cols, preferred_element_type=jnp.float32)
    cdf = 0.5 * (1.0 + lax.erf(pre * 0.7071067811865476))
    hidden = (pre * cdf).astype(jnp.bfloat16)
    back_hidden = jnp.dot(branch_all, w_out_cols_t, preferred_element_type=jnp.float32)
    density = jnp.exp(-0.5 * pre * pre) * 0.3989422804014327
    hidden_grad = (back_hidden * (cdf + pre * density)).astype(jnp.bfloat16)
    scale = 1.0 / float(images * tile_rows * tile_cols * n_rows * n_cols) ** 0.5
    out_terms_t = lax.dot_general(
        branch_all, hidden, (((0,), (0,)), ((), ())), preferred_element_type=jnp.float32
    )
    in_terms = lax.dot_general(
        normed_all, hidden_grad, (((0,), (0,)), ((), ())), preferred_element_type=jnp.float32
    )
    grad_w2 = (scatter_split(out_terms_t) * scale).T
    grad_w1 = scatter_split(in_terms) * scale
    normed_grad = scatter_rows(
        lax.dot_general(
            hidden_grad, w_in_cols, (((1,), (1,)), ((), ())), preferred_element_type=jnp.float32
        ),
        "cols",
        (0, 1)[:col_bits],
    )
    gain_applied = (
        normed_grad.reshape(images, tile_rows, tile_cols, channel_total) * layer_norm_gain
    )
    convolution_gradient = inverse_deviation * (
        gain_applied
        - jnp.mean(gain_applied, axis=-1, keepdims=True)
        - standardized_input * jnp.mean(gain_applied * standardized_input, axis=-1, keepdims=True)
    )
    grad_t = to_tiles(convolution_gradient)
    kernel_rows = []
    for r in range(kernel_size):
        row_terms = []
        for s in range(kernel_size):
            term = jnp.sum(
                grad_t * padded[r : r + tile_rows, s : s + tile_cols].astype(jnp.float32),
                axis=(0, 1),
            )
            row_terms.append(term.reshape(images, channel_total).sum(axis=0))
        kernel_rows.append(jnp.stack(row_terms))
    grad_kernel = jnp.stack(kernel_rows)
    for bit in range(col_bits):
        grad_kernel = grad_kernel + swap_with(grad_kernel, "cols", bit)
    for bit in (0, 1, 3, 2, 4)[:row_bits]:
        grad_kernel = grad_kernel + swap_with(grad_kernel, "rows", bit)
    grad_kernel = grad_kernel * scale
    grad_pad = with_halo(grad_t, (("rows", 0), ("cols", 1)), kernel_reach)
    total = to_tiles(out_grad).astype(jnp.float32)
    for r in range(kernel_size):
        for s in range(kernel_size):
            row_from = 2 * kernel_reach - r
            col_from = 2 * kernel_reach - s
            total = (
                total
                + taps[r, s]
                * grad_pad[row_from : row_from + tile_rows, col_from : col_from + tile_cols]
            )
    total = from_tiles(total)
    input_grad = total.astype(jnp.bfloat16)
    return (input_grad, grad_w1, grad_w2, grad_kernel)


def solution(mesh):
    return jax.shard_map(
        local,
        mesh=mesh,
        in_specs=(
            P(None, "rows", "cols", None),
            P(None, ("rows", "cols"), None),
            P(),
            P(),
            P("rows", "cols"),
            P("cols", "rows"),
            P(),
        ),
        out_specs=(P(None, "rows", "cols", None), P("rows", "cols"), P("cols", "rows"), P()),
        check_vma=False,
    )
```

```python
import jax
import jax.numpy as jnp
from jax import lax
from jax.sharding import PartitionSpec as P


def with_halo(value, sides, width):
    for axis, dim in sides:
        peers, length = (lax.axis_size(axis), value.shape[dim])
        up = [(i, (i + 1) % peers) for i in range(peers - 1)]
        down = [(j, i) for i, j in up]
        last = lax.slice_in_dim(value, length - width, length, axis=dim)
        first = lax.slice_in_dim(value, 0, width, axis=dim)
        before = lax.ppermute(last, axis, up)
        after = lax.ppermute(first, axis, down)
        value = jnp.concatenate([before, value, after], axis=dim)
    return value


def swap_with(value, axis, bit):
    peers = lax.axis_size(axis)
    return lax.ppermute(value, axis, [(i, i ^ (1 << bit)) for i in range(peers)])


def gather_rows(value, axis, order):
    me = lax.axis_index(axis)
    for bit in order:
        other = swap_with(value, axis, bit)
        b = (me >> bit) & 1
        both = jnp.concatenate([value, other, value], axis=0)
        value = lax.dynamic_slice_in_dim(both, b * value.shape[0], 2 * value.shape[0], axis=0)
    n = len(order)
    block = value.shape[0] >> n
    rest = value.shape[1:]
    value = value.reshape((2,) * n + (block,) + rest)
    perm = [n - 1 - order.index(k) for k in reversed(range(n))]
    value = value.transpose(perm + list(range(n, value.ndim)))
    return value.reshape((block << n,) + rest)


def scatter_rows(value, axis, order):
    me = lax.axis_index(axis)
    n = len(order)
    block = value.shape[0] >> n
    rest = value.shape[1:]
    value = value.reshape((2,) * n + (block,) + rest)
    perm = [n - 1 - order[j] for j in range(n)]
    value = value.transpose(perm + list(range(n, value.ndim))).reshape((block << n,) + rest)
    for bit in order:
        half = value.shape[0] // 2
        b = (me >> bit) & 1
        keep = lax.dynamic_slice_in_dim(value, b * half, half, axis=0)
        send = lax.dynamic_slice_in_dim(value, (1 - b) * half, half, axis=0)
        value = keep + swap_with(send, axis, bit)
    return value


GATHER_ORDERS = ((4, 2, 3, 1, 0), (2, 4, 0, 3, 1), (4, 2, 1, 0, 3))
SCATTER_ORDERS = ((0, 1, 3, 2, 4), (1, 3, 0, 4, 2), (3, 0, 1, 2, 4))


def scatter_split(value):
    third = value.shape[1] // 3
    return jnp.concatenate(
        [
            scatter_rows(value[:, i * third : (i + 1) * third], "rows", order)
            for i, order in enumerate(SCATTER_ORDERS)
        ],
        axis=1,
    )


def local(block_input, token_grads, conv_kernel, layer_norm_gain, w_in, w_out, layer_scale):
    images, tile_rows, tile_cols, channel_total = block_input.shape
    kernel_size = conv_kernel.shape[0]
    kernel_reach = kernel_size // 2
    n_rows = lax.axis_size("rows")
    n_cols = lax.axis_size("cols")
    row_bits = n_rows.bit_length() - 1
    col_bits = n_cols.bit_length() - 1
    run_count = tile_rows // 2
    half_cols = tile_cols // 2
    col_index = lax.axis_index("cols")

    hidden_cols = w_in.shape[1]
    both_weights = jnp.concatenate([w_in, w_out.T], axis=1)
    third = both_weights.shape[1] // 3
    gathered = jnp.concatenate(
        [
            gather_rows(both_weights[:, i * third : (i + 1) * third], "rows", order)
            for i, order in enumerate(GATHER_ORDERS)
        ],
        axis=1,
    )
    w_in_cols = gathered[:, :hidden_cols]
    w_out_cols_t = gathered[:, hidden_cols:]

    tokens = token_grads.reshape(images, 2, half_cols, 4 * channel_total)
    first_half = col_index // 2
    send_a = lax.dynamic_index_in_dim(tokens, first_half, 1, keepdims=False)
    send_b = lax.dynamic_index_in_dim(tokens, 1 - first_half, 1, keepdims=False)
    got_a = lax.ppermute(send_a, "cols", [(s, 2 * (s % 2) + s // 2) for s in range(n_cols)])
    got_b = lax.ppermute(send_b, "cols", [(s, 2 * (s % 2) + 1 - s // 2) for s in range(n_cols)])
    merged = lax.dynamic_slice_in_dim(
        jnp.stack([got_a, got_b, got_a], axis=1), col_index % 2, 2, axis=1
    )
    out_grad = merged.reshape(images, run_count, half_cols, 2, 2, channel_total)
    out_grad = out_grad.transpose(0, 1, 3, 2, 4, 5).reshape(
        images, tile_rows, tile_cols, channel_total
    )
    pixel_total = images * tile_rows * tile_cols
    branch_grad = (
        (out_grad.astype(jnp.float32) * layer_scale)
        .astype(jnp.bfloat16)
        .reshape(pixel_total, channel_total)
    )
    branch_all = lax.all_gather(branch_grad, "cols", axis=0, tiled=True)
    lane = 128
    groups = channel_total // lane

    def to_tiles(x):
        x = x.reshape(images, tile_rows, tile_cols, groups, lane).transpose(1, 2, 0, 3, 4)
        return x.reshape(tile_rows, tile_cols, images * groups, lane)

    def from_tiles(t):
        t = t.reshape(tile_rows, tile_cols, images, groups, lane).transpose(2, 0, 1, 3, 4)
        return t.reshape(images, tile_rows, tile_cols, channel_total)

    taps = jnp.tile(
        conv_kernel.reshape(kernel_size, kernel_size, 1, groups, lane), (1, 1, images, 1, 1)
    ).reshape(kernel_size, kernel_size, images * groups, lane)
    padded = with_halo(to_tiles(block_input), (("rows", 0), ("cols", 1)), kernel_reach)
    w_in_cols, w_out_cols_t, padded = lax.optimization_barrier((w_in_cols, w_out_cols_t, padded))
    conv_t = jnp.zeros((tile_rows, tile_cols, images * groups, lane), jnp.float32)
    for r in range(kernel_size):
        for s in range(kernel_size):
            conv_t = conv_t + taps[r, s] * padded[r : r + tile_rows, s : s + tile_cols].astype(
                jnp.float32
            )
    conv_out = from_tiles(conv_t)
    mean_val = jnp.mean(conv_out, axis=-1, keepdims=True)
    centered_input = conv_out - mean_val
    var_val = jnp.mean(centered_input * centered_input, axis=-1, keepdims=True)
    inverse_deviation = lax.rsqrt(var_val + 1e-06)
    standardized_input = centered_input * inverse_deviation
    norm_output = (
        (standardized_input * layer_norm_gain)
        .astype(jnp.bfloat16)
        .reshape(pixel_total, channel_total)
    )
    normed_all = lax.all_gather(norm_output, "cols", axis=0, tiled=True)
    pre = jnp.dot(normed_all, w_in_cols, preferred_element_type=jnp.float32)
    cdf = 0.5 * (1.0 + lax.erf(pre * 0.7071067811865476))
    hidden = (pre * cdf).astype(jnp.bfloat16)
    back_hidden = jnp.dot(branch_all, w_out_cols_t, preferred_element_type=jnp.float32)
    density = jnp.exp(-0.5 * pre * pre) * 0.3989422804014327
    hidden_grad = (back_hidden * (cdf + pre * density)).astype(jnp.bfloat16)
    scale = 1.0 / float(images * tile_rows * tile_cols * n_rows * n_cols) ** 0.5
    out_terms_t = lax.dot_general(
        branch_all, hidden, (((0,), (0,)), ((), ())), preferred_element_type=jnp.float32
    )
    in_terms = lax.dot_general(
        normed_all, hidden_grad, (((0,), (0,)), ((), ())), preferred_element_type=jnp.float32
    )
    grad_w2 = (scatter_split(out_terms_t) * scale).T
    grad_w1 = scatter_split(in_terms) * scale
    normed_grad = lax.psum_scatter(
        lax.dot_general(
            hidden_grad, w_in_cols, (((1,), (1,)), ((), ())), preferred_element_type=jnp.float32
        ),
        "cols",
        scatter_dimension=0,
        tiled=True,
    )
    gain_applied = (
        normed_grad.reshape(images, tile_rows, tile_cols, channel_total) * layer_norm_gain
    )
    convolution_gradient = inverse_deviation * (
        gain_applied
        - jnp.mean(gain_applied, axis=-1, keepdims=True)
        - standardized_input * jnp.mean(gain_applied * standardized_input, axis=-1, keepdims=True)
    )
    grad_t = to_tiles(convolution_gradient)
    kernel_rows = []
    for r in range(kernel_size):
        row_terms = []
        for s in range(kernel_size):
            term = jnp.sum(
                grad_t * padded[r : r + tile_rows, s : s + tile_cols].astype(jnp.float32),
                axis=(0, 1),
            )
            row_terms.append(term.reshape(images, channel_total).sum(axis=0))
        kernel_rows.append(jnp.stack(row_terms))
    grad_kernel = jnp.stack(kernel_rows).reshape(kernel_size * kernel_size * channel_total)
    col_order = tuple(range(col_bits))
    row_order = (0, 1, 3, 2, 4)[:row_bits]
    pieces = 1 << (col_bits + row_bits)
    grad_kernel = grad_kernel.reshape(pieces, -1)
    grad_kernel = scatter_rows(grad_kernel, "cols", col_order)
    grad_kernel = scatter_rows(grad_kernel, "rows", row_order)
    grad_kernel = gather_rows(grad_kernel, "rows", row_order[::-1])
    grad_kernel = gather_rows(grad_kernel, "cols", col_order[::-1])
    grad_kernel = grad_kernel.reshape(kernel_size, kernel_size, channel_total) * scale
    grad_pad = with_halo(grad_t, (("rows", 0), ("cols", 1)), kernel_reach)
    total = to_tiles(out_grad).astype(jnp.float32)
    for r in range(kernel_size):
        for s in range(kernel_size):
            row_from = 2 * kernel_reach - r
            col_from = 2 * kernel_reach - s
            total = (
                total
                + taps[r, s]
                * grad_pad[row_from : row_from + tile_rows, col_from : col_from + tile_cols]
            )
    total = from_tiles(total)
    input_grad = total.astype(jnp.bfloat16)
    return (input_grad, grad_w1, grad_w2, grad_kernel)


def solution(mesh):
    return jax.shard_map(
        local,
        mesh=mesh,
        in_specs=(
            P(None, "rows", "cols", None),
            P(None, ("rows", "cols"), None),
            P(),
            P(),
            P("rows", "cols"),
            P("cols", "rows"),
            P(),
        ),
        out_specs=(P(None, "rows", "cols", None), P("rows", "cols"), P("cols", "rows"), P()),
        check_vma=False,
    )
```

```python
import jax
import jax.numpy as jnp
from jax import lax
from jax.sharding import PartitionSpec as P


def with_halo(value, sides, width):
    for axis, dim in sides:
        peers, length = (lax.axis_size(axis), value.shape[dim])
        up = [(i, (i + 1) % peers) for i in range(peers - 1)]
        down = [(j, i) for i, j in up]
        last = lax.slice_in_dim(value, length - width, length, axis=dim)
        first = lax.slice_in_dim(value, 0, width, axis=dim)
        before = lax.ppermute(last, axis, up)
        after = lax.ppermute(first, axis, down)
        value = jnp.concatenate([before, value, after], axis=dim)
    return value


def swap_with(value, axis, bit):
    peers = lax.axis_size(axis)
    return lax.ppermute(value, axis, [(i, i ^ (1 << bit)) for i in range(peers)])


def gather_rows(value, axis, order):
    me = lax.axis_index(axis)
    for bit in order:
        other = swap_with(value, axis, bit)
        b = (me >> bit) & 1
        both = jnp.concatenate([value, other, value], axis=0)
        value = lax.dynamic_slice_in_dim(both, b * value.shape[0], 2 * value.shape[0], axis=0)
    n = len(order)
    block = value.shape[0] >> n
    rest = value.shape[1:]
    value = value.reshape((2,) * n + (block,) + rest)
    perm = [n - 1 - order.index(k) for k in reversed(range(n))]
    value = value.transpose(perm + list(range(n, value.ndim)))
    return value.reshape((block << n,) + rest)


def scatter_rows(value, axis, order, narrow_steps=0):
    me = lax.axis_index(axis)
    n = len(order)
    block = value.shape[0] >> n
    rest = value.shape[1:]
    value = value.reshape((2,) * n + (block,) + rest)
    perm = [n - 1 - order[j] for j in range(n)]
    value = value.transpose(perm + list(range(n, value.ndim))).reshape((block << n,) + rest)
    for step, bit in enumerate(order):
        half = value.shape[0] // 2
        b = (me >> bit) & 1
        keep = lax.dynamic_slice_in_dim(value, b * half, half, axis=0)
        send = lax.dynamic_slice_in_dim(value, (1 - b) * half, half, axis=0)
        if step < narrow_steps:
            got = swap_with(send.astype(jnp.bfloat16), axis, bit).astype(value.dtype)
        else:
            got = swap_with(send, axis, bit)
        value = keep + got
    return value


GATHER_ORDERS = ((4, 2, 3, 1, 0), (2, 4, 0, 3, 1), (4, 2, 1, 0, 3))
SCATTER_ORDERS = ((0, 1, 3, 2, 4), (1, 3, 0, 4, 2), (3, 0, 1, 2, 4))


def scatter_split(value):
    third = value.shape[1] // 3
    return jnp.concatenate(
        [
            scatter_rows(value[:, i * third : (i + 1) * third], "rows", order, 2)
            for i, order in enumerate(SCATTER_ORDERS)
        ],
        axis=1,
    )


def local(block_input, token_grads, conv_kernel, layer_norm_gain, w_in, w_out, layer_scale):
    images, tile_rows, tile_cols, channel_total = block_input.shape
    kernel_size = conv_kernel.shape[0]
    kernel_reach = kernel_size // 2
    n_rows = lax.axis_size("rows")
    n_cols = lax.axis_size("cols")
    row_bits = n_rows.bit_length() - 1
    col_bits = n_cols.bit_length() - 1
    run_count = tile_rows // 2
    half_cols = tile_cols // 2
    col_index = lax.axis_index("cols")

    hidden_cols = w_in.shape[1]
    both_weights = jnp.concatenate([w_in, w_out.T], axis=1)
    third = both_weights.shape[1] // 3
    gathered = jnp.concatenate(
        [
            gather_rows(both_weights[:, i * third : (i + 1) * third], "rows", order)
            for i, order in enumerate(GATHER_ORDERS)
        ],
        axis=1,
    )
    w_in_cols = gathered[:, :hidden_cols]
    w_out_cols_t = gathered[:, hidden_cols:]

    tokens = token_grads.reshape(images, 2, half_cols, 4 * channel_total)
    first_half = col_index // 2
    send_a = lax.dynamic_index_in_dim(tokens, first_half, 1, keepdims=False)
    send_b = lax.dynamic_index_in_dim(tokens, 1 - first_half, 1, keepdims=False)
    got_a = lax.ppermute(send_a, "cols", [(s, 2 * (s % 2) + s // 2) for s in range(n_cols)])
    got_b = lax.ppermute(send_b, "cols", [(s, 2 * (s % 2) + 1 - s // 2) for s in range(n_cols)])
    merged = lax.dynamic_slice_in_dim(
        jnp.stack([got_a, got_b, got_a], axis=1), col_index % 2, 2, axis=1
    )
    out_grad = merged.reshape(images, run_count, half_cols, 2, 2, channel_total)
    out_grad = out_grad.transpose(0, 1, 3, 2, 4, 5).reshape(
        images, tile_rows, tile_cols, channel_total
    )
    pixel_total = images * tile_rows * tile_cols
    branch_grad = (
        (out_grad.astype(jnp.float32) * layer_scale)
        .astype(jnp.bfloat16)
        .reshape(pixel_total, channel_total)
    )
    lane = 128
    groups = channel_total // lane

    def to_tiles(x):
        x = x.reshape(images, tile_rows, tile_cols, groups, lane).transpose(1, 2, 0, 3, 4)
        return x.reshape(tile_rows, tile_cols, images * groups, lane)

    def from_tiles(t):
        t = t.reshape(tile_rows, tile_cols, images, groups, lane).transpose(2, 0, 1, 3, 4)
        return t.reshape(images, tile_rows, tile_cols, channel_total)

    taps = jnp.tile(
        conv_kernel.reshape(kernel_size, kernel_size, 1, groups, lane), (1, 1, images, 1, 1)
    ).reshape(kernel_size, kernel_size, images * groups, lane)
    padded = with_halo(to_tiles(block_input), (("rows", 0), ("cols", 1)), kernel_reach)
    w_in_cols, w_out_cols_t, branch_grad, padded = lax.optimization_barrier(
        (w_in_cols, w_out_cols_t, branch_grad, padded)
    )
    branch_all = lax.all_gather(branch_grad, "cols", axis=0, tiled=True)
    conv_t = jnp.zeros((tile_rows, tile_cols, images * groups, lane), jnp.float32)
    for r in range(kernel_size):
        for s in range(kernel_size):
            conv_t = conv_t + taps[r, s] * padded[r : r + tile_rows, s : s + tile_cols].astype(
                jnp.float32
            )
    conv_out = from_tiles(conv_t)
    mean_val = jnp.mean(conv_out, axis=-1, keepdims=True)
    centered_input = conv_out - mean_val
    var_val = jnp.mean(centered_input * centered_input, axis=-1, keepdims=True)
    inverse_deviation = lax.rsqrt(var_val + 1e-06)
    standardized_input = centered_input * inverse_deviation
    norm_output = (
        (standardized_input * layer_norm_gain)
        .astype(jnp.bfloat16)
        .reshape(pixel_total, channel_total)
    )
    normed_all = lax.all_gather(norm_output, "cols", axis=0, tiled=True)
    pre = jnp.dot(normed_all, w_in_cols, preferred_element_type=jnp.float32)
    cdf = 0.5 * (1.0 + lax.erf(pre * 0.7071067811865476))
    hidden = (pre * cdf).astype(jnp.bfloat16)
    back_hidden = jnp.dot(branch_all, w_out_cols_t, preferred_element_type=jnp.float32)
    density = jnp.exp(-0.5 * pre * pre) * 0.3989422804014327
    hidden_grad = (back_hidden * (cdf + pre * density)).astype(jnp.bfloat16)
    scale = 1.0 / float(images * tile_rows * tile_cols * n_rows * n_cols) ** 0.5
    out_terms_t = lax.dot_general(
        branch_all, hidden, (((0,), (0,)), ((), ())), preferred_element_type=jnp.float32
    )
    in_terms = lax.dot_general(
        normed_all, hidden_grad, (((0,), (0,)), ((), ())), preferred_element_type=jnp.float32
    )
    grad_w2 = (scatter_split(out_terms_t) * scale).T
    grad_w1 = scatter_split(in_terms) * scale
    normed_grad = lax.psum_scatter(
        lax.dot_general(
            hidden_grad, w_in_cols, (((1,), (1,)), ((), ())), preferred_element_type=jnp.float32
        ),
        "cols",
        scatter_dimension=0,
        tiled=True,
    )
    gain_applied = (
        normed_grad.reshape(images, tile_rows, tile_cols, channel_total) * layer_norm_gain
    )
    convolution_gradient = inverse_deviation * (
        gain_applied
        - jnp.mean(gain_applied, axis=-1, keepdims=True)
        - standardized_input * jnp.mean(gain_applied * standardized_input, axis=-1, keepdims=True)
    )
    grad_t = to_tiles(convolution_gradient)
    kernel_rows = []
    for r in range(kernel_size):
        row_terms = []
        for s in range(kernel_size):
            term = jnp.sum(
                grad_t * padded[r : r + tile_rows, s : s + tile_cols].astype(jnp.float32),
                axis=(0, 1),
            )
            row_terms.append(term.reshape(images, channel_total).sum(axis=0))
        kernel_rows.append(jnp.stack(row_terms))
    grad_kernel = jnp.stack(kernel_rows).reshape(kernel_size * kernel_size * channel_total)
    col_order = tuple(range(col_bits))
    row_order = (0, 1, 3, 2, 4)[:row_bits]
    pieces = 1 << (col_bits + row_bits)
    grad_kernel = grad_kernel.reshape(pieces, -1)
    grad_kernel = scatter_rows(grad_kernel, "cols", col_order)
    grad_kernel = scatter_rows(grad_kernel, "rows", row_order)
    grad_kernel = gather_rows(grad_kernel, "rows", row_order[::-1])
    grad_kernel = gather_rows(grad_kernel, "cols", col_order[::-1])
    grad_kernel = grad_kernel.reshape(kernel_size, kernel_size, channel_total) * scale
    grad_pad = with_halo(grad_t, (("rows", 0), ("cols", 1)), kernel_reach)
    total = to_tiles(out_grad).astype(jnp.float32)
    for r in range(kernel_size):
        for s in range(kernel_size):
            row_from = 2 * kernel_reach - r
            col_from = 2 * kernel_reach - s
            total = (
                total
                + taps[r, s]
                * grad_pad[row_from : row_from + tile_rows, col_from : col_from + tile_cols]
            )
    total = from_tiles(total)
    input_grad = total.astype(jnp.bfloat16)
    return (input_grad, grad_w1, grad_w2, grad_kernel)


def solution(mesh):
    return jax.shard_map(
        local,
        mesh=mesh,
        in_specs=(
            P(None, "rows", "cols", None),
            P(None, ("rows", "cols"), None),
            P(),
            P(),
            P("rows", "cols"),
            P("cols", "rows"),
            P(),
        ),
        out_specs=(P(None, "rows", "cols", None), P("rows", "cols"), P("cols", "rows"), P()),
        check_vma=False,
    )
```

```python
import jax
import jax.numpy as jnp
from jax import lax
from jax.sharding import PartitionSpec as P


def with_halo(value, sides, width, link_dtype=None):
    link_dtype = link_dtype or value.dtype
    for axis, dim in sides:
        peers, length = (lax.axis_size(axis), value.shape[dim])
        up = [(i, (i + 1) % peers) for i in range(peers - 1)]
        down = [(j, i) for i, j in up]
        last = lax.slice_in_dim(value, length - width, length, axis=dim).astype(link_dtype)
        first = lax.slice_in_dim(value, 0, width, axis=dim).astype(link_dtype)
        before = lax.ppermute(last, axis, up).astype(value.dtype)
        after = lax.ppermute(first, axis, down).astype(value.dtype)
        value = jnp.concatenate([before, value, after], axis=dim)
    return value


def swap_with(value, axis, bit):
    peers = lax.axis_size(axis)
    return lax.ppermute(value, axis, [(i, i ^ (1 << bit)) for i in range(peers)])


def gather_rows(value, axis, order):
    me = lax.axis_index(axis)
    for bit in order:
        other = swap_with(value, axis, bit)
        b = (me >> bit) & 1
        both = jnp.concatenate([value, other, value], axis=0)
        value = lax.dynamic_slice_in_dim(both, b * value.shape[0], 2 * value.shape[0], axis=0)
    n = len(order)
    block = value.shape[0] >> n
    rest = value.shape[1:]
    value = value.reshape((2,) * n + (block,) + rest)
    perm = [n - 1 - order.index(k) for k in reversed(range(n))]
    value = value.transpose(perm + list(range(n, value.ndim)))
    return value.reshape((block << n,) + rest)


def scatter_rows(value, axis, order, narrow_steps=0):
    me = lax.axis_index(axis)
    n = len(order)
    block = value.shape[0] >> n
    rest = value.shape[1:]
    value = value.reshape((2,) * n + (block,) + rest)
    perm = [n - 1 - order[j] for j in range(n)]
    value = value.transpose(perm + list(range(n, value.ndim))).reshape((block << n,) + rest)
    for step, bit in enumerate(order):
        half = value.shape[0] // 2
        b = (me >> bit) & 1
        keep = lax.dynamic_slice_in_dim(value, b * half, half, axis=0)
        send = lax.dynamic_slice_in_dim(value, (1 - b) * half, half, axis=0)
        if step < narrow_steps:
            got = swap_with(send.astype(jnp.bfloat16), axis, bit).astype(value.dtype)
        else:
            got = swap_with(send, axis, bit)
        value = keep + got
    return value


GATHER_ORDERS = ((4, 2, 3, 1, 0), (2, 4, 0, 3, 1), (4, 2, 1, 0, 3))
SCATTER_ORDERS = ((0, 1, 3, 2, 4), (1, 3, 0, 4, 2), (3, 0, 1, 2, 4))


def scatter_split(value):
    third = value.shape[1] // 3
    return jnp.concatenate(
        [
            scatter_rows(value[:, i * third : (i + 1) * third], "rows", order, 2)
            for i, order in enumerate(SCATTER_ORDERS)
        ],
        axis=1,
    )


def local(block_input, token_grads, conv_kernel, layer_norm_gain, w_in, w_out, layer_scale):
    images, tile_rows, tile_cols, channel_total = block_input.shape
    kernel_size = conv_kernel.shape[0]
    kernel_reach = kernel_size // 2
    n_rows = lax.axis_size("rows")
    n_cols = lax.axis_size("cols")
    row_bits = n_rows.bit_length() - 1
    col_bits = n_cols.bit_length() - 1
    run_count = tile_rows // 2
    half_cols = tile_cols // 2
    col_index = lax.axis_index("cols")

    hidden_cols = w_in.shape[1]
    both_weights = jnp.concatenate([w_in, w_out.T], axis=1)
    third = both_weights.shape[1] // 3
    gathered = jnp.concatenate(
        [
            gather_rows(both_weights[:, i * third : (i + 1) * third], "rows", order)
            for i, order in enumerate(GATHER_ORDERS)
        ],
        axis=1,
    )
    w_in_cols = gathered[:, :hidden_cols]
    w_out_cols_t = gathered[:, hidden_cols:]

    tokens = token_grads.reshape(images, 2, half_cols, 4 * channel_total)
    first_half = col_index // 2
    send_a = lax.dynamic_index_in_dim(tokens, first_half, 1, keepdims=False)
    send_b = lax.dynamic_index_in_dim(tokens, 1 - first_half, 1, keepdims=False)
    got_a = lax.ppermute(send_a, "cols", [(s, 2 * (s % 2) + s // 2) for s in range(n_cols)])
    got_b = lax.ppermute(send_b, "cols", [(s, 2 * (s % 2) + 1 - s // 2) for s in range(n_cols)])
    merged = lax.dynamic_slice_in_dim(
        jnp.stack([got_a, got_b, got_a], axis=1), col_index % 2, 2, axis=1
    )
    out_grad = merged.reshape(images, run_count, half_cols, 2, 2, channel_total)
    out_grad = out_grad.transpose(0, 1, 3, 2, 4, 5).reshape(
        images, tile_rows, tile_cols, channel_total
    )
    pixel_total = images * tile_rows * tile_cols
    branch_grad = (
        (out_grad.astype(jnp.float32) * layer_scale)
        .astype(jnp.bfloat16)
        .reshape(pixel_total, channel_total)
    )
    lane = 128
    groups = channel_total // lane

    def to_tiles(x):
        x = x.reshape(images, tile_rows, tile_cols, groups, lane).transpose(1, 2, 0, 3, 4)
        return x.reshape(tile_rows, tile_cols, images * groups, lane)

    def from_tiles(t):
        t = t.reshape(tile_rows, tile_cols, images, groups, lane).transpose(2, 0, 1, 3, 4)
        return t.reshape(images, tile_rows, tile_cols, channel_total)

    taps = jnp.tile(
        conv_kernel.reshape(kernel_size, kernel_size, 1, groups, lane), (1, 1, images, 1, 1)
    ).reshape(kernel_size, kernel_size, images * groups, lane)
    padded = with_halo(to_tiles(block_input), (("rows", 0), ("cols", 1)), kernel_reach)
    branch_all = lax.all_gather(branch_grad, "cols", axis=0, tiled=True)
    w_in_cols, w_out_cols_t, branch_all, padded = lax.optimization_barrier(
        (w_in_cols, w_out_cols_t, branch_all, padded)
    )
    conv_t = jnp.zeros((tile_rows, tile_cols, images * groups, lane), jnp.float32)
    for r in range(kernel_size):
        for s in range(kernel_size):
            conv_t = conv_t + taps[r, s] * padded[r : r + tile_rows, s : s + tile_cols].astype(
                jnp.float32
            )
    conv_out = from_tiles(conv_t)
    mean_val = jnp.mean(conv_out, axis=-1, keepdims=True)
    centered_input = conv_out - mean_val
    var_val = jnp.mean(centered_input * centered_input, axis=-1, keepdims=True)
    inverse_deviation = lax.rsqrt(var_val + 1e-06)
    standardized_input = centered_input * inverse_deviation
    norm_output = (
        (standardized_input * layer_norm_gain)
        .astype(jnp.bfloat16)
        .reshape(pixel_total, channel_total)
    )
    normed_all = lax.all_gather(norm_output, "cols", axis=0, tiled=True)
    pre = jnp.dot(normed_all, w_in_cols, preferred_element_type=jnp.float32)
    cdf = 0.5 * (1.0 + lax.erf(pre * 0.7071067811865476))
    hidden = (pre * cdf).astype(jnp.bfloat16)
    back_hidden = jnp.dot(branch_all, w_out_cols_t, preferred_element_type=jnp.float32)
    density = jnp.exp(-0.5 * pre * pre) * 0.3989422804014327
    hidden_grad = (back_hidden * (cdf + pre * density)).astype(jnp.bfloat16)
    scale = 1.0 / float(images * tile_rows * tile_cols * n_rows * n_cols) ** 0.5
    out_terms_t = lax.dot_general(
        branch_all, hidden, (((0,), (0,)), ((), ())), preferred_element_type=jnp.float32
    )
    in_terms = lax.dot_general(
        normed_all, hidden_grad, (((0,), (0,)), ((), ())), preferred_element_type=jnp.float32
    )
    grad_w2 = (scatter_split(out_terms_t) * scale).T
    grad_w1 = scatter_split(in_terms) * scale
    normed_grad = scatter_rows(
        lax.dot_general(
            hidden_grad, w_in_cols, (((1,), (1,)), ((), ())), preferred_element_type=jnp.float32
        ),
        "cols",
        (0, 1)[:col_bits],
        col_bits,
    )
    gain_applied = (
        normed_grad.reshape(images, tile_rows, tile_cols, channel_total) * layer_norm_gain
    )
    convolution_gradient = inverse_deviation * (
        gain_applied
        - jnp.mean(gain_applied, axis=-1, keepdims=True)
        - standardized_input * jnp.mean(gain_applied * standardized_input, axis=-1, keepdims=True)
    )
    grad_t = to_tiles(convolution_gradient)
    kernel_rows = []
    for r in range(kernel_size):
        row_terms = []
        for s in range(kernel_size):
            term = jnp.sum(
                grad_t * padded[r : r + tile_rows, s : s + tile_cols].astype(jnp.float32),
                axis=(0, 1),
            )
            row_terms.append(term.reshape(images, channel_total).sum(axis=0))
        kernel_rows.append(jnp.stack(row_terms))
    grad_kernel = jnp.stack(kernel_rows).reshape(kernel_size * kernel_size * channel_total)
    col_order = tuple(range(col_bits))
    row_order = (0, 1, 3, 2, 4)[:row_bits]
    pieces = 1 << (col_bits + row_bits)
    grad_kernel = grad_kernel.reshape(pieces, -1)
    grad_kernel = scatter_rows(grad_kernel, "cols", col_order)
    grad_kernel = scatter_rows(grad_kernel, "rows", row_order)
    grad_kernel = gather_rows(grad_kernel, "rows", row_order[::-1])
    grad_kernel = gather_rows(grad_kernel, "cols", col_order[::-1])
    grad_kernel = grad_kernel.reshape(kernel_size, kernel_size, channel_total) * scale
    grad_pad = with_halo(grad_t, (("rows", 0), ("cols", 1)), kernel_reach, jnp.bfloat16)
    total = to_tiles(out_grad).astype(jnp.float32)
    for r in range(kernel_size):
        for s in range(kernel_size):
            row_from = 2 * kernel_reach - r
            col_from = 2 * kernel_reach - s
            total = (
                total
                + taps[r, s]
                * grad_pad[row_from : row_from + tile_rows, col_from : col_from + tile_cols]
            )
    total = from_tiles(total)
    input_grad = total.astype(jnp.bfloat16)
    return (input_grad, grad_w1, grad_w2, grad_kernel)


def solution(mesh):
    return jax.shard_map(
        local,
        mesh=mesh,
        in_specs=(
            P(None, "rows", "cols", None),
            P(None, ("rows", "cols"), None),
            P(),
            P(),
            P("rows", "cols"),
            P("cols", "rows"),
            P(),
        ),
        out_specs=(P(None, "rows", "cols", None), P("rows", "cols"), P("cols", "rows"), P()),
        check_vma=False,
    )
```

```python
import jax
import jax.numpy as jnp
from jax import lax
from jax.sharding import PartitionSpec as P


def with_halo(value, sides, width, link_dtype=None):
    link_dtype = link_dtype or value.dtype
    for axis, dim in sides:
        peers, length = (lax.axis_size(axis), value.shape[dim])
        up = [(i, (i + 1) % peers) for i in range(peers - 1)]
        down = [(j, i) for i, j in up]
        last = lax.slice_in_dim(value, length - width, length, axis=dim).astype(link_dtype)
        first = lax.slice_in_dim(value, 0, width, axis=dim).astype(link_dtype)
        before = lax.ppermute(last, axis, up).astype(value.dtype)
        after = lax.ppermute(first, axis, down).astype(value.dtype)
        value = jnp.concatenate([before, value, after], axis=dim)
    return value


def swap_with(value, axis, bit):
    peers = lax.axis_size(axis)
    return lax.ppermute(value, axis, [(i, i ^ (1 << bit)) for i in range(peers)])


def gather_rows(value, axis, order):
    me = lax.axis_index(axis)
    for bit in order:
        other = swap_with(value, axis, bit)
        b = (me >> bit) & 1
        both = jnp.concatenate([value, other, value], axis=0)
        value = lax.dynamic_slice_in_dim(both, b * value.shape[0], 2 * value.shape[0], axis=0)
    n = len(order)
    block = value.shape[0] >> n
    rest = value.shape[1:]
    value = value.reshape((2,) * n + (block,) + rest)
    perm = [n - 1 - order.index(k) for k in reversed(range(n))]
    value = value.transpose(perm + list(range(n, value.ndim)))
    return value.reshape((block << n,) + rest)


def scatter_rows(value, axis, order, narrow_steps=0):
    me = lax.axis_index(axis)
    n = len(order)
    block = value.shape[0] >> n
    rest = value.shape[1:]
    value = value.reshape((2,) * n + (block,) + rest)
    perm = [n - 1 - order[j] for j in range(n)]
    value = value.transpose(perm + list(range(n, value.ndim))).reshape((block << n,) + rest)
    for step, bit in enumerate(order):
        half = value.shape[0] // 2
        b = (me >> bit) & 1
        keep = lax.dynamic_slice_in_dim(value, b * half, half, axis=0)
        send = lax.dynamic_slice_in_dim(value, (1 - b) * half, half, axis=0)
        if step < narrow_steps:
            got = swap_with(send.astype(jnp.bfloat16), axis, bit).astype(value.dtype)
        else:
            got = swap_with(send, axis, bit)
        value = keep + got
    return value


GATHER_ORDERS = ((4, 2, 3, 1, 0), (2, 4, 0, 3, 1), (4, 2, 1, 0, 3))
SCATTER_ORDERS = ((0, 1, 3, 2, 4), (1, 3, 0, 4, 2), (3, 0, 1, 2, 4))


def scatter_split(value):
    third = value.shape[1] // 3
    return jnp.concatenate(
        [
            scatter_rows(value[:, i * third : (i + 1) * third], "rows", order, 2)
            for i, order in enumerate(SCATTER_ORDERS)
        ],
        axis=1,
    )


def local(block_input, token_grads, conv_kernel, layer_norm_gain, w_in, w_out, layer_scale):
    images, tile_rows, tile_cols, channel_total = block_input.shape
    kernel_size = conv_kernel.shape[0]
    kernel_reach = kernel_size // 2
    n_rows = lax.axis_size("rows")
    n_cols = lax.axis_size("cols")
    row_bits = n_rows.bit_length() - 1
    col_bits = n_cols.bit_length() - 1
    run_count = tile_rows // 2
    half_cols = tile_cols // 2
    col_index = lax.axis_index("cols")

    tokens = token_grads.reshape(images, 2, half_cols, 4 * channel_total)
    first_half = col_index // 2
    send_a = lax.dynamic_index_in_dim(tokens, first_half, 1, keepdims=False)
    send_b = lax.dynamic_index_in_dim(tokens, 1 - first_half, 1, keepdims=False)
    got_a = lax.ppermute(send_a, "cols", [(s, 2 * (s % 2) + s // 2) for s in range(n_cols)])
    got_b = lax.ppermute(send_b, "cols", [(s, 2 * (s % 2) + 1 - s // 2) for s in range(n_cols)])
    merged = lax.dynamic_slice_in_dim(
        jnp.stack([got_a, got_b, got_a], axis=1), col_index % 2, 2, axis=1
    )
    out_grad = merged.reshape(images, run_count, half_cols, 2, 2, channel_total)
    out_grad = out_grad.transpose(0, 1, 3, 2, 4, 5).reshape(
        images, tile_rows, tile_cols, channel_total
    )
    pixel_total = images * tile_rows * tile_cols
    branch_grad = (
        (out_grad.astype(jnp.float32) * layer_scale)
        .astype(jnp.bfloat16)
        .reshape(pixel_total, channel_total)
    )
    lane = 128
    groups = channel_total // lane

    def to_tiles(x):
        x = x.reshape(images, tile_rows, tile_cols, groups, lane).transpose(1, 2, 0, 3, 4)
        return x.reshape(tile_rows, tile_cols, images * groups, lane)

    def from_tiles(t):
        t = t.reshape(tile_rows, tile_cols, images, groups, lane).transpose(2, 0, 1, 3, 4)
        return t.reshape(images, tile_rows, tile_cols, channel_total)

    taps = jnp.tile(
        conv_kernel.reshape(kernel_size, kernel_size, 1, groups, lane), (1, 1, images, 1, 1)
    ).reshape(kernel_size, kernel_size, images * groups, lane)
    padded = with_halo(to_tiles(block_input), (("rows", 0), ("cols", 1)), kernel_reach)
    branch_all = lax.all_gather(branch_grad, "cols", axis=0, tiled=True)
    conv_t = jnp.zeros((tile_rows, tile_cols, images * groups, lane), jnp.float32)
    for r in range(kernel_size):
        for s in range(kernel_size):
            conv_t = conv_t + taps[r, s] * padded[r : r + tile_rows, s : s + tile_cols].astype(
                jnp.float32
            )
    conv_out = from_tiles(conv_t)
    mean_val = jnp.mean(conv_out, axis=-1, keepdims=True)
    centered_input = conv_out - mean_val
    var_val = jnp.mean(centered_input * centered_input, axis=-1, keepdims=True)
    inverse_deviation = lax.rsqrt(var_val + 1e-06)
    standardized_input = centered_input * inverse_deviation
    norm_output = (
        (standardized_input * layer_norm_gain)
        .astype(jnp.bfloat16)
        .reshape(pixel_total, channel_total)
    )
    hidden_cols = w_in.shape[1]
    both_weights = jnp.concatenate([w_in, w_out.T], axis=1)
    both_weights, norm_output = lax.optimization_barrier((both_weights, norm_output))
    third = both_weights.shape[1] // 3
    gathered = jnp.concatenate(
        [
            gather_rows(both_weights[:, i * third : (i + 1) * third], "rows", order)
            for i, order in enumerate(GATHER_ORDERS)
        ],
        axis=1,
    )
    w_in_cols = gathered[:, :hidden_cols]
    w_out_cols_t = gathered[:, hidden_cols:]

    normed_all = lax.all_gather(norm_output, "cols", axis=0, tiled=True)
    pre = jnp.dot(normed_all, w_in_cols, preferred_element_type=jnp.float32)
    cdf = 0.5 * (1.0 + lax.erf(pre * 0.7071067811865476))
    hidden = (pre * cdf).astype(jnp.bfloat16)
    back_hidden = jnp.dot(branch_all, w_out_cols_t, preferred_element_type=jnp.float32)
    density = jnp.exp(-0.5 * pre * pre) * 0.3989422804014327
    hidden_grad = (back_hidden * (cdf + pre * density)).astype(jnp.bfloat16)
    scale = 1.0 / float(images * tile_rows * tile_cols * n_rows * n_cols) ** 0.5
    out_terms_t = lax.dot_general(
        branch_all, hidden, (((0,), (0,)), ((), ())), preferred_element_type=jnp.float32
    )
    in_terms = lax.dot_general(
        normed_all, hidden_grad, (((0,), (0,)), ((), ())), preferred_element_type=jnp.float32
    )
    grad_w2 = (scatter_split(out_terms_t) * scale).T
    grad_w1 = scatter_split(in_terms) * scale
    normed_grad = scatter_rows(
        lax.dot_general(
            hidden_grad, w_in_cols, (((1,), (1,)), ((), ())), preferred_element_type=jnp.float32
        ),
        "cols",
        (0, 1)[:col_bits],
        col_bits,
    )
    gain_applied = (
        normed_grad.reshape(images, tile_rows, tile_cols, channel_total) * layer_norm_gain
    )
    convolution_gradient = inverse_deviation * (
        gain_applied
        - jnp.mean(gain_applied, axis=-1, keepdims=True)
        - standardized_input * jnp.mean(gain_applied * standardized_input, axis=-1, keepdims=True)
    )
    grad_t = to_tiles(convolution_gradient)
    kernel_rows = []
    for r in range(kernel_size):
        row_terms = []
        for s in range(kernel_size):
            term = jnp.sum(
                grad_t * padded[r : r + tile_rows, s : s + tile_cols].astype(jnp.float32),
                axis=(0, 1),
            )
            row_terms.append(term.reshape(images, channel_total).sum(axis=0))
        kernel_rows.append(jnp.stack(row_terms))
    grad_kernel = jnp.stack(kernel_rows).reshape(kernel_size * kernel_size * channel_total)
    col_order = tuple(range(col_bits))
    row_order = (0, 1, 3, 2, 4)[:row_bits]
    pieces = 1 << col_bits
    grad_kernel = grad_kernel.reshape(pieces, -1)
    grad_kernel = scatter_rows(grad_kernel, "cols", col_order)
    for bit in row_order:
        grad_kernel = grad_kernel + swap_with(grad_kernel, "rows", bit)
    grad_kernel = gather_rows(grad_kernel, "cols", col_order[::-1])
    grad_kernel = grad_kernel.reshape(kernel_size, kernel_size, channel_total) * scale
    grad_pad = with_halo(grad_t, (("rows", 0), ("cols", 1)), kernel_reach, jnp.bfloat16)
    total = to_tiles(out_grad).astype(jnp.float32)
    for r in range(kernel_size):
        for s in range(kernel_size):
            row_from = 2 * kernel_reach - r
            col_from = 2 * kernel_reach - s
            total = (
                total
                + taps[r, s]
                * grad_pad[row_from : row_from + tile_rows, col_from : col_from + tile_cols]
            )
    total = from_tiles(total)
    input_grad = total.astype(jnp.bfloat16)
    return (input_grad, grad_w1, grad_w2, grad_kernel)


def solution(mesh):
    return jax.shard_map(
        local,
        mesh=mesh,
        in_specs=(
            P(None, "rows", "cols", None),
            P(None, ("rows", "cols"), None),
            P(),
            P(),
            P("rows", "cols"),
            P("cols", "rows"),
            P(),
        ),
        out_specs=(P(None, "rows", "cols", None), P("rows", "cols"), P("cols", "rows"), P()),
        check_vma=False,
    )
```

```python
import jax
import jax.numpy as jnp
from jax import lax
from jax.sharding import PartitionSpec as P


def with_halo(value, sides, width, link_dtype=None):
    link_dtype = link_dtype or value.dtype
    for axis, dim in sides:
        peers, length = (lax.axis_size(axis), value.shape[dim])
        up = [(i, (i + 1) % peers) for i in range(peers - 1)]
        down = [(j, i) for i, j in up]
        last = lax.slice_in_dim(value, length - width, length, axis=dim).astype(link_dtype)
        first = lax.slice_in_dim(value, 0, width, axis=dim).astype(link_dtype)
        before = lax.ppermute(last, axis, up).astype(value.dtype)
        after = lax.ppermute(first, axis, down).astype(value.dtype)
        value = jnp.concatenate([before, value, after], axis=dim)
    return value


def swap_with(value, axis, bit):
    peers = lax.axis_size(axis)
    return lax.ppermute(value, axis, [(i, i ^ (1 << bit)) for i in range(peers)])


def gather_rows(value, axis, order):
    me = lax.axis_index(axis)
    for bit in order:
        other = swap_with(value, axis, bit)
        b = (me >> bit) & 1
        both = jnp.concatenate([value, other, value], axis=0)
        value = lax.dynamic_slice_in_dim(both, b * value.shape[0], 2 * value.shape[0], axis=0)
    n = len(order)
    block = value.shape[0] >> n
    rest = value.shape[1:]
    value = value.reshape((2,) * n + (block,) + rest)
    perm = [n - 1 - order.index(k) for k in reversed(range(n))]
    value = value.transpose(perm + list(range(n, value.ndim)))
    return value.reshape((block << n,) + rest)


def gather_direct(value, axis):
    peers = lax.axis_size(axis)
    me = lax.axis_index(axis)
    got = [value] + [
        lax.ppermute(value, axis, [(i, i ^ k) for i in range(peers)]) for k in range(1, peers)
    ]
    stacked = jnp.stack(got)
    order = jnp.bitwise_xor(me, jnp.arange(peers, dtype=me.dtype))
    picked = jnp.take(stacked, order, axis=0)
    return picked.reshape((peers * value.shape[0],) + value.shape[1:])


def scatter_rows(value, axis, order, narrow_steps=0):
    me = lax.axis_index(axis)
    n = len(order)
    block = value.shape[0] >> n
    rest = value.shape[1:]
    value = value.reshape((2,) * n + (block,) + rest)
    perm = [n - 1 - order[j] for j in range(n)]
    value = value.transpose(perm + list(range(n, value.ndim))).reshape((block << n,) + rest)
    for step, bit in enumerate(order):
        half = value.shape[0] // 2
        b = (me >> bit) & 1
        keep = lax.dynamic_slice_in_dim(value, b * half, half, axis=0)
        send = lax.dynamic_slice_in_dim(value, (1 - b) * half, half, axis=0)
        if step < narrow_steps:
            got = swap_with(send.astype(jnp.bfloat16), axis, bit).astype(value.dtype)
        else:
            got = swap_with(send, axis, bit)
        value = keep + got
    return value


GATHER_ORDERS = ((4, 2, 3, 1, 0), (2, 4, 0, 3, 1), (4, 2, 1, 0, 3))
SCATTER_ORDERS = ((0, 1, 3, 2, 4), (1, 3, 0, 4, 2), (3, 0, 1, 2, 4))


def scatter_split(value):
    third = value.shape[1] // 3
    return jnp.concatenate(
        [
            scatter_rows(value[:, i * third : (i + 1) * third], "rows", order, 2)
            for i, order in enumerate(SCATTER_ORDERS)
        ],
        axis=1,
    )


def local(block_input, token_grads, conv_kernel, layer_norm_gain, w_in, w_out, layer_scale):
    images, tile_rows, tile_cols, channel_total = block_input.shape
    kernel_size = conv_kernel.shape[0]
    kernel_reach = kernel_size // 2
    n_rows = lax.axis_size("rows")
    n_cols = lax.axis_size("cols")
    row_bits = n_rows.bit_length() - 1
    col_bits = n_cols.bit_length() - 1
    run_count = tile_rows // 2
    half_cols = tile_cols // 2
    col_index = lax.axis_index("cols")

    hidden_cols = w_in.shape[1]
    both_weights = jnp.concatenate([w_in, w_out.T], axis=1)
    gathered = gather_direct(both_weights, "rows")
    w_in_cols = gathered[:, :hidden_cols]
    w_out_cols_t = gathered[:, hidden_cols:]

    tokens = token_grads.reshape(images, 2, half_cols, 4 * channel_total)
    first_half = col_index // 2
    send_a = lax.dynamic_index_in_dim(tokens, first_half, 1, keepdims=False)
    send_b = lax.dynamic_index_in_dim(tokens, 1 - first_half, 1, keepdims=False)
    got_a = lax.ppermute(send_a, "cols", [(s, 2 * (s % 2) + s // 2) for s in range(n_cols)])
    got_b = lax.ppermute(send_b, "cols", [(s, 2 * (s % 2) + 1 - s // 2) for s in range(n_cols)])
    merged = lax.dynamic_slice_in_dim(
        jnp.stack([got_a, got_b, got_a], axis=1), col_index % 2, 2, axis=1
    )
    out_grad = merged.reshape(images, run_count, half_cols, 2, 2, channel_total)
    out_grad = out_grad.transpose(0, 1, 3, 2, 4, 5).reshape(
        images, tile_rows, tile_cols, channel_total
    )
    pixel_total = images * tile_rows * tile_cols
    branch_grad = (
        (out_grad.astype(jnp.float32) * layer_scale)
        .astype(jnp.bfloat16)
        .reshape(pixel_total, channel_total)
    )
    lane = 128
    groups = channel_total // lane

    def to_tiles(x):
        x = x.reshape(images, tile_rows, tile_cols, groups, lane).transpose(1, 2, 0, 3, 4)
        return x.reshape(tile_rows, tile_cols, images * groups, lane)

    def from_tiles(t):
        t = t.reshape(tile_rows, tile_cols, images, groups, lane).transpose(2, 0, 1, 3, 4)
        return t.reshape(images, tile_rows, tile_cols, channel_total)

    taps = jnp.tile(
        conv_kernel.reshape(kernel_size, kernel_size, 1, groups, lane), (1, 1, images, 1, 1)
    ).reshape(kernel_size, kernel_size, images * groups, lane)
    padded = with_halo(to_tiles(block_input), (("rows", 0), ("cols", 1)), kernel_reach)
    branch_all = lax.all_gather(branch_grad, "cols", axis=0, tiled=True)
    conv_t = jnp.zeros((tile_rows, tile_cols, images * groups, lane), jnp.float32)
    for r in range(kernel_size):
        for s in range(kernel_size):
            conv_t = conv_t + taps[r, s] * padded[r : r + tile_rows, s : s + tile_cols].astype(
                jnp.float32
            )
    conv_out = from_tiles(conv_t)
    mean_val = jnp.mean(conv_out, axis=-1, keepdims=True)
    centered_input = conv_out - mean_val
    var_val = jnp.mean(centered_input * centered_input, axis=-1, keepdims=True)
    inverse_deviation = lax.rsqrt(var_val + 1e-06)
    standardized_input = centered_input * inverse_deviation
    norm_output = (
        (standardized_input * layer_norm_gain)
        .astype(jnp.bfloat16)
        .reshape(pixel_total, channel_total)
    )
    normed_all = lax.all_gather(norm_output, "cols", axis=0, tiled=True)
    pre = jnp.dot(normed_all, w_in_cols, preferred_element_type=jnp.float32)
    cdf = 0.5 * (1.0 + lax.erf(pre * 0.7071067811865476))
    hidden = (pre * cdf).astype(jnp.bfloat16)
    back_hidden = jnp.dot(branch_all, w_out_cols_t, preferred_element_type=jnp.float32)
    density = jnp.exp(-0.5 * pre * pre) * 0.3989422804014327
    hidden_grad = (back_hidden * (cdf + pre * density)).astype(jnp.bfloat16)
    scale = 1.0 / float(images * tile_rows * tile_cols * n_rows * n_cols) ** 0.5
    out_terms_t = lax.dot_general(
        branch_all, hidden, (((0,), (0,)), ((), ())), preferred_element_type=jnp.float32
    )
    in_terms = lax.dot_general(
        normed_all, hidden_grad, (((0,), (0,)), ((), ())), preferred_element_type=jnp.float32
    )
    grad_w2 = (scatter_split(out_terms_t) * scale).T
    grad_w1 = scatter_split(in_terms) * scale
    normed_grad = scatter_rows(
        lax.dot_general(
            hidden_grad, w_in_cols, (((1,), (1,)), ((), ())), preferred_element_type=jnp.float32
        ),
        "cols",
        (0, 1)[:col_bits],
        col_bits,
    )
    gain_applied = (
        normed_grad.reshape(images, tile_rows, tile_cols, channel_total) * layer_norm_gain
    )
    convolution_gradient = inverse_deviation * (
        gain_applied
        - jnp.mean(gain_applied, axis=-1, keepdims=True)
        - standardized_input * jnp.mean(gain_applied * standardized_input, axis=-1, keepdims=True)
    )
    grad_t = to_tiles(convolution_gradient)
    kernel_rows = []
    for r in range(kernel_size):
        row_terms = []
        for s in range(kernel_size):
            term = jnp.sum(
                grad_t * padded[r : r + tile_rows, s : s + tile_cols].astype(jnp.float32),
                axis=(0, 1),
            )
            row_terms.append(term.reshape(images, channel_total).sum(axis=0))
        kernel_rows.append(jnp.stack(row_terms))
    grad_kernel = jnp.stack(kernel_rows).reshape(kernel_size * kernel_size * channel_total)
    col_order = tuple(range(col_bits))
    row_order = (0, 1, 3, 2, 4)[:row_bits]
    pieces = 1 << (col_bits + row_bits)
    grad_kernel = grad_kernel.reshape(pieces, -1)
    grad_kernel = scatter_rows(grad_kernel, "cols", col_order)
    grad_kernel = scatter_rows(grad_kernel, "rows", row_order)
    grad_kernel = gather_rows(grad_kernel, "rows", row_order[::-1])
    grad_kernel = gather_rows(grad_kernel, "cols", col_order[::-1])
    grad_kernel = grad_kernel.reshape(kernel_size, kernel_size, channel_total) * scale
    grad_pad = with_halo(grad_t, (("rows", 0), ("cols", 1)), kernel_reach, jnp.bfloat16)
    total = to_tiles(out_grad).astype(jnp.float32)
    for r in range(kernel_size):
        for s in range(kernel_size):
            row_from = 2 * kernel_reach - r
            col_from = 2 * kernel_reach - s
            total = (
                total
                + taps[r, s]
                * grad_pad[row_from : row_from + tile_rows, col_from : col_from + tile_cols]
            )
    total = from_tiles(total)
    input_grad = total.astype(jnp.bfloat16)
    return (input_grad, grad_w1, grad_w2, grad_kernel)


def solution(mesh):
    return jax.shard_map(
        local,
        mesh=mesh,
        in_specs=(
            P(None, "rows", "cols", None),
            P(None, ("rows", "cols"), None),
            P(),
            P(),
            P("rows", "cols"),
            P("cols", "rows"),
            P(),
        ),
        out_specs=(P(None, "rows", "cols", None), P("rows", "cols"), P("cols", "rows"), P()),
        check_vma=False,
    )
```

```python
import jax
import jax.numpy as jnp
from jax import lax
from jax.sharding import PartitionSpec as P


def with_halo(value, sides, width, link_dtype=None):
    link_dtype = link_dtype or value.dtype
    for axis, dim in sides:
        peers, length = (lax.axis_size(axis), value.shape[dim])
        up = [(i, (i + 1) % peers) for i in range(peers - 1)]
        down = [(j, i) for i, j in up]
        last = lax.slice_in_dim(value, length - width, length, axis=dim).astype(link_dtype)
        first = lax.slice_in_dim(value, 0, width, axis=dim).astype(link_dtype)
        before = lax.ppermute(last, axis, up).astype(value.dtype)
        after = lax.ppermute(first, axis, down).astype(value.dtype)
        value = jnp.concatenate([before, value, after], axis=dim)
    return value


def swap_with(value, axis, bit):
    peers = lax.axis_size(axis)
    return lax.ppermute(value, axis, [(i, i ^ (1 << bit)) for i in range(peers)])


def gather_rows(value, axis, order):
    me = lax.axis_index(axis)
    for bit in order:
        other = swap_with(value, axis, bit)
        b = (me >> bit) & 1
        both = jnp.concatenate([value, other, value], axis=0)
        value = lax.dynamic_slice_in_dim(both, b * value.shape[0], 2 * value.shape[0], axis=0)
    n = len(order)
    block = value.shape[0] >> n
    rest = value.shape[1:]
    value = value.reshape((2,) * n + (block,) + rest)
    perm = [n - 1 - order.index(k) for k in reversed(range(n))]
    value = value.transpose(perm + list(range(n, value.ndim)))
    return value.reshape((block << n,) + rest)


def scatter_rows(value, axis, order, narrow_steps=0):
    me = lax.axis_index(axis)
    n = len(order)
    block = value.shape[0] >> n
    rest = value.shape[1:]
    value = value.reshape((2,) * n + (block,) + rest)
    perm = [n - 1 - order[j] for j in range(n)]
    value = value.transpose(perm + list(range(n, value.ndim))).reshape((block << n,) + rest)
    for step, bit in enumerate(order):
        half = value.shape[0] // 2
        b = (me >> bit) & 1
        keep = lax.dynamic_slice_in_dim(value, b * half, half, axis=0)
        send = lax.dynamic_slice_in_dim(value, (1 - b) * half, half, axis=0)
        if step < narrow_steps:
            got = swap_with(send.astype(jnp.bfloat16), axis, bit).astype(value.dtype)
        else:
            got = swap_with(send, axis, bit)
        value = keep + got
    return value


GATHER_ORDERS = ((4, 2, 3, 1, 0), (2, 4, 0, 3, 1), (4, 2, 1, 0, 3))
SCATTER_ORDERS = ((0, 1, 3, 2, 4), (1, 3, 0, 4, 2), (3, 0, 1, 2, 4))


def scatter_split(value):
    third = value.shape[1] // 3
    return jnp.concatenate(
        [
            scatter_rows(value[:, i * third : (i + 1) * third], "rows", order, 2)
            for i, order in enumerate(SCATTER_ORDERS)
        ],
        axis=1,
    )


def local(block_input, token_grads, conv_kernel, layer_norm_gain, w_in, w_out, layer_scale):
    images, tile_rows, tile_cols, channel_total = block_input.shape
    kernel_size = conv_kernel.shape[0]
    kernel_reach = kernel_size // 2
    n_rows = lax.axis_size("rows")
    n_cols = lax.axis_size("cols")
    row_bits = n_rows.bit_length() - 1
    col_bits = n_cols.bit_length() - 1
    run_count = tile_rows // 2
    half_cols = tile_cols // 2
    col_index = lax.axis_index("cols")

    hidden_cols = w_in.shape[1]
    both_weights = jnp.concatenate([w_in, w_out.T], axis=1)
    third = both_weights.shape[1] // 3
    gathered = jnp.concatenate(
        [
            gather_rows(both_weights[:, i * third : (i + 1) * third], "rows", order)
            for i, order in enumerate(GATHER_ORDERS)
        ],
        axis=1,
    )
    w_in_cols = gathered[:, :hidden_cols]
    w_out_cols_t = gathered[:, hidden_cols:]

    tokens = token_grads.reshape(images, 2, half_cols, 4 * channel_total)
    first_half = col_index // 2
    send_a = lax.dynamic_index_in_dim(tokens, first_half, 1, keepdims=False)
    send_b = lax.dynamic_index_in_dim(tokens, 1 - first_half, 1, keepdims=False)
    got_a = lax.ppermute(send_a, "cols", [(s, 2 * (s % 2) + s // 2) for s in range(n_cols)])
    got_b = lax.ppermute(send_b, "cols", [(s, 2 * (s % 2) + 1 - s // 2) for s in range(n_cols)])
    merged = lax.dynamic_slice_in_dim(
        jnp.stack([got_a, got_b, got_a], axis=1), col_index % 2, 2, axis=1
    )
    out_grad = merged.reshape(images, run_count, half_cols, 2, 2, channel_total)
    out_grad = out_grad.transpose(0, 1, 3, 2, 4, 5).reshape(
        images, tile_rows, tile_cols, channel_total
    )
    pixel_total = images * tile_rows * tile_cols
    branch_grad = (
        (out_grad.astype(jnp.float32) * layer_scale)
        .astype(jnp.bfloat16)
        .reshape(pixel_total, channel_total)
    )
    lane = 128
    groups = channel_total // lane

    def to_tiles(x):
        x = x.reshape(images, tile_rows, tile_cols, groups, lane).transpose(1, 2, 0, 3, 4)
        return x.reshape(tile_rows, tile_cols, images * groups, lane)

    def from_tiles(t):
        t = t.reshape(tile_rows, tile_cols, images, groups, lane).transpose(2, 0, 1, 3, 4)
        return t.reshape(images, tile_rows, tile_cols, channel_total)

    taps = jnp.tile(
        conv_kernel.reshape(kernel_size, kernel_size, 1, groups, lane), (1, 1, images, 1, 1)
    ).reshape(kernel_size, kernel_size, images * groups, lane)
    padded = with_halo(to_tiles(block_input), (("rows", 0), ("cols", 1)), kernel_reach)
    branch_all = lax.all_gather(branch_grad, "cols", axis=0, tiled=True)
    w_in_cols, w_out_cols_t, branch_all, padded = lax.optimization_barrier(
        (w_in_cols, w_out_cols_t, branch_all, padded)
    )
    conv_t = jnp.zeros((tile_rows, tile_cols, images * groups, lane), jnp.float32)
    for r in range(kernel_size):
        for s in range(kernel_size):
            conv_t = conv_t + taps[r, s] * padded[r : r + tile_rows, s : s + tile_cols].astype(
                jnp.float32
            )
    conv_out = from_tiles(conv_t)
    mean_val = jnp.mean(conv_out, axis=-1, keepdims=True)
    centered_input = conv_out - mean_val
    var_val = jnp.mean(centered_input * centered_input, axis=-1, keepdims=True)
    inverse_deviation = lax.rsqrt(var_val + 1e-06)
    standardized_input = centered_input * inverse_deviation
    norm_output = (
        (standardized_input * layer_norm_gain)
        .astype(jnp.bfloat16)
        .reshape(pixel_total, channel_total)
    )
    normed_all = gather_rows(norm_output, "cols", (1, 0)[:col_bits])
    pre = jnp.dot(normed_all, w_in_cols, preferred_element_type=jnp.float32)
    cdf = 0.5 * (1.0 + lax.erf(pre * 0.7071067811865476))
    hidden = (pre * cdf).astype(jnp.bfloat16)
    back_hidden = jnp.dot(branch_all, w_out_cols_t, preferred_element_type=jnp.float32)
    density = jnp.exp(-0.5 * pre * pre) * 0.3989422804014327
    hidden_grad = (back_hidden * (cdf + pre * density)).astype(jnp.bfloat16)
    scale = 1.0 / float(images * tile_rows * tile_cols * n_rows * n_cols) ** 0.5
    out_terms_t = lax.dot_general(
        branch_all, hidden, (((0,), (0,)), ((), ())), preferred_element_type=jnp.float32
    )
    in_terms = lax.dot_general(
        normed_all, hidden_grad, (((0,), (0,)), ((), ())), preferred_element_type=jnp.float32
    )
    grad_w2 = (scatter_split(out_terms_t) * scale).T
    grad_w1 = scatter_split(in_terms) * scale
    normed_grad = scatter_rows(
        lax.dot_general(
            hidden_grad, w_in_cols, (((1,), (1,)), ((), ())), preferred_element_type=jnp.float32
        ),
        "cols",
        (0, 1)[:col_bits],
        col_bits,
    )
    gain_applied = (
        normed_grad.reshape(images, tile_rows, tile_cols, channel_total) * layer_norm_gain
    )
    convolution_gradient = inverse_deviation * (
        gain_applied
        - jnp.mean(gain_applied, axis=-1, keepdims=True)
        - standardized_input * jnp.mean(gain_applied * standardized_input, axis=-1, keepdims=True)
    )
    grad_t = to_tiles(convolution_gradient)
    kernel_rows = []
    for r in range(kernel_size):
        row_terms = []
        for s in range(kernel_size):
            term = jnp.sum(
                grad_t * padded[r : r + tile_rows, s : s + tile_cols].astype(jnp.float32),
                axis=(0, 1),
            )
            row_terms.append(term.reshape(images, channel_total).sum(axis=0))
        kernel_rows.append(jnp.stack(row_terms))
    grad_kernel = jnp.stack(kernel_rows).reshape(kernel_size * kernel_size * channel_total)
    col_order = tuple(range(col_bits))
    row_order = (0, 1, 3, 2, 4)[:row_bits]
    pieces = 1 << (col_bits + row_bits)
    grad_kernel = grad_kernel.reshape(pieces, -1)
    grad_kernel = scatter_rows(grad_kernel, "cols", col_order)
    grad_kernel = scatter_rows(grad_kernel, "rows", row_order)
    grad_kernel = gather_rows(grad_kernel, "rows", row_order[::-1])
    grad_kernel = gather_rows(grad_kernel, "cols", col_order[::-1])
    grad_kernel = grad_kernel.reshape(kernel_size, kernel_size, channel_total) * scale
    grad_pad = with_halo(grad_t, (("rows", 0), ("cols", 1)), kernel_reach, jnp.bfloat16)
    total = to_tiles(out_grad).astype(jnp.float32)
    for r in range(kernel_size):
        for s in range(kernel_size):
            row_from = 2 * kernel_reach - r
            col_from = 2 * kernel_reach - s
            total = (
                total
                + taps[r, s]
                * grad_pad[row_from : row_from + tile_rows, col_from : col_from + tile_cols]
            )
    total = from_tiles(total)
    input_grad = total.astype(jnp.bfloat16)
    return (input_grad, grad_w1, grad_w2, grad_kernel)


def solution(mesh):
    return jax.shard_map(
        local,
        mesh=mesh,
        in_specs=(
            P(None, "rows", "cols", None),
            P(None, ("rows", "cols"), None),
            P(),
            P(),
            P("rows", "cols"),
            P("cols", "rows"),
            P(),
        ),
        out_specs=(P(None, "rows", "cols", None), P("rows", "cols"), P("cols", "rows"), P()),
        check_vma=False,
    )
```

```python
import jax
import jax.numpy as jnp
from jax import lax
from jax.sharding import PartitionSpec as P


def with_halo(value, sides, width, link_dtype=None):
    link_dtype = link_dtype or value.dtype
    for axis, dim in sides:
        peers, length = (lax.axis_size(axis), value.shape[dim])
        up = [(i, (i + 1) % peers) for i in range(peers - 1)]
        down = [(j, i) for i, j in up]
        last = lax.slice_in_dim(value, length - width, length, axis=dim).astype(link_dtype)
        first = lax.slice_in_dim(value, 0, width, axis=dim).astype(link_dtype)
        before = lax.ppermute(last, axis, up).astype(value.dtype)
        after = lax.ppermute(first, axis, down).astype(value.dtype)
        value = jnp.concatenate([before, value, after], axis=dim)
    return value


def swap_with(value, axis, bit):
    peers = lax.axis_size(axis)
    return lax.ppermute(value, axis, [(i, i ^ (1 << bit)) for i in range(peers)])


def gather_rows(value, axis, order, direct_bits=()):
    me = lax.axis_index(axis)
    if direct_bits:
        peers = lax.axis_size(axis)
        masks = [sum(1 << b for j, b in enumerate(direct_bits) if (m >> j) & 1)
                 for m in range(1 << len(direct_bits))]
        got = [value] + [
            lax.ppermute(value, axis, [(i, i ^ mask) for i in range(peers)]) for mask in masks[1:]
        ]
        local = sum(((me >> b) & 1) << j for j, b in enumerate(direct_bits))
        stacked = jnp.stack(got)
        pick = jnp.bitwise_xor(local, jnp.arange(len(masks), dtype=me.dtype))
        value = jnp.take(stacked, pick, axis=0).reshape((-1,) + value.shape[1:])
    for bit in order[len(direct_bits):]:
        other = swap_with(value, axis, bit)
        b = (me >> bit) & 1
        both = jnp.concatenate([value, other, value], axis=0)
        value = lax.dynamic_slice_in_dim(both, b * value.shape[0], 2 * value.shape[0], axis=0)
    n = len(order)
    block = value.shape[0] >> n
    rest = value.shape[1:]
    value = value.reshape((2,) * n + (block,) + rest)
    perm = [n - 1 - order.index(k) for k in reversed(range(n))]
    value = value.transpose(perm + list(range(n, value.ndim)))
    return value.reshape((block << n,) + rest)


def scatter_rows(value, axis, order, narrow_steps=0):
    me = lax.axis_index(axis)
    n = len(order)
    block = value.shape[0] >> n
    rest = value.shape[1:]
    value = value.reshape((2,) * n + (block,) + rest)
    perm = [n - 1 - order[j] for j in range(n)]
    value = value.transpose(perm + list(range(n, value.ndim))).reshape((block << n,) + rest)
    for step, bit in enumerate(order):
        half = value.shape[0] // 2
        b = (me >> bit) & 1
        keep = lax.dynamic_slice_in_dim(value, b * half, half, axis=0)
        send = lax.dynamic_slice_in_dim(value, (1 - b) * half, half, axis=0)
        if step < narrow_steps:
            got = swap_with(send.astype(jnp.bfloat16), axis, bit).astype(value.dtype)
        else:
            got = swap_with(send, axis, bit)
        value = keep + got
    return value


GATHER_ORDERS = ((4, 2, 3, 1, 0), (2, 4, 0, 3, 1), (4, 2, 1, 0, 3))
SCATTER_ORDERS = ((0, 1, 3, 2, 4), (1, 3, 0, 4, 2), (3, 0, 1, 2, 4))


def scatter_split(value):
    third = value.shape[1] // 3
    return jnp.concatenate(
        [
            scatter_rows(value[:, i * third : (i + 1) * third], "rows", order, 2)
            for i, order in enumerate(SCATTER_ORDERS)
        ],
        axis=1,
    )


def local(block_input, token_grads, conv_kernel, layer_norm_gain, w_in, w_out, layer_scale):
    images, tile_rows, tile_cols, channel_total = block_input.shape
    kernel_size = conv_kernel.shape[0]
    kernel_reach = kernel_size // 2
    n_rows = lax.axis_size("rows")
    n_cols = lax.axis_size("cols")
    row_bits = n_rows.bit_length() - 1
    col_bits = n_cols.bit_length() - 1
    run_count = tile_rows // 2
    half_cols = tile_cols // 2
    col_index = lax.axis_index("cols")

    hidden_cols = w_in.shape[1]
    both_weights = jnp.concatenate([w_in, w_out.T], axis=1)
    third = both_weights.shape[1] // 3
    gathered = jnp.concatenate(
        [
            gather_rows(both_weights[:, i * third : (i + 1) * third], "rows", order, order[:2])
            for i, order in enumerate(GATHER_ORDERS)
        ],
        axis=1,
    )
    w_in_cols = gathered[:, :hidden_cols]
    w_out_cols_t = gathered[:, hidden_cols:]

    tokens = token_grads.reshape(images, 2, half_cols, 4 * channel_total)
    first_half = col_index // 2
    send_a = lax.dynamic_index_in_dim(tokens, first_half, 1, keepdims=False)
    send_b = lax.dynamic_index_in_dim(tokens, 1 - first_half, 1, keepdims=False)
    got_a = lax.ppermute(send_a, "cols", [(s, 2 * (s % 2) + s // 2) for s in range(n_cols)])
    got_b = lax.ppermute(send_b, "cols", [(s, 2 * (s % 2) + 1 - s // 2) for s in range(n_cols)])
    merged = lax.dynamic_slice_in_dim(
        jnp.stack([got_a, got_b, got_a], axis=1), col_index % 2, 2, axis=1
    )
    out_grad = merged.reshape(images, run_count, half_cols, 2, 2, channel_total)
    out_grad = out_grad.transpose(0, 1, 3, 2, 4, 5).reshape(
        images, tile_rows, tile_cols, channel_total
    )
    pixel_total = images * tile_rows * tile_cols
    branch_grad = (
        (out_grad.astype(jnp.float32) * layer_scale)
        .astype(jnp.bfloat16)
        .reshape(pixel_total, channel_total)
    )
    lane = 128
    groups = channel_total // lane

    def to_tiles(x):
        x = x.reshape(images, tile_rows, tile_cols, groups, lane).transpose(1, 2, 0, 3, 4)
        return x.reshape(tile_rows, tile_cols, images * groups, lane)

    def from_tiles(t):
        t = t.reshape(tile_rows, tile_cols, images, groups, lane).transpose(2, 0, 1, 3, 4)
        return t.reshape(images, tile_rows, tile_cols, channel_total)

    taps = jnp.tile(
        conv_kernel.reshape(kernel_size, kernel_size, 1, groups, lane), (1, 1, images, 1, 1)
    ).reshape(kernel_size, kernel_size, images * groups, lane)
    padded = with_halo(to_tiles(block_input), (("rows", 0), ("cols", 1)), kernel_reach)
    branch_all = lax.all_gather(branch_grad, "cols", axis=0, tiled=True)
    w_in_cols, w_out_cols_t, branch_all, padded = lax.optimization_barrier(
        (w_in_cols, w_out_cols_t, branch_all, padded)
    )
    conv_t = jnp.zeros((tile_rows, tile_cols, images * groups, lane), jnp.float32)
    for r in range(kernel_size):
        for s in range(kernel_size):
            conv_t = conv_t + taps[r, s] * padded[r : r + tile_rows, s : s + tile_cols].astype(
                jnp.float32
            )
    conv_out = from_tiles(conv_t)
    mean_val = jnp.mean(conv_out, axis=-1, keepdims=True)
    centered_input = conv_out - mean_val
    var_val = jnp.mean(centered_input * centered_input, axis=-1, keepdims=True)
    inverse_deviation = lax.rsqrt(var_val + 1e-06)
    standardized_input = centered_input * inverse_deviation
    norm_output = (
        (standardized_input * layer_norm_gain)
        .astype(jnp.bfloat16)
        .reshape(pixel_total, channel_total)
    )
    normed_all = lax.all_gather(norm_output, "cols", axis=0, tiled=True)
    pre = jnp.dot(normed_all, w_in_cols, preferred_element_type=jnp.float32)
    cdf = 0.5 * (1.0 + lax.erf(pre * 0.7071067811865476))
    hidden = (pre * cdf).astype(jnp.bfloat16)
    back_hidden = jnp.dot(branch_all, w_out_cols_t, preferred_element_type=jnp.float32)
    density = jnp.exp(-0.5 * pre * pre) * 0.3989422804014327
    hidden_grad = (back_hidden * (cdf + pre * density)).astype(jnp.bfloat16)
    scale = 1.0 / float(images * tile_rows * tile_cols * n_rows * n_cols) ** 0.5
    out_terms_t = lax.dot_general(
        branch_all, hidden, (((0,), (0,)), ((), ())), preferred_element_type=jnp.float32
    )
    in_terms = lax.dot_general(
        normed_all, hidden_grad, (((0,), (0,)), ((), ())), preferred_element_type=jnp.float32
    )
    grad_w2 = (scatter_split(out_terms_t) * scale).T
    grad_w1 = scatter_split(in_terms) * scale
    normed_grad = scatter_rows(
        lax.dot_general(
            hidden_grad, w_in_cols, (((1,), (1,)), ((), ())), preferred_element_type=jnp.float32
        ),
        "cols",
        (0, 1)[:col_bits],
        col_bits,
    )
    gain_applied = (
        normed_grad.reshape(images, tile_rows, tile_cols, channel_total) * layer_norm_gain
    )
    convolution_gradient = inverse_deviation * (
        gain_applied
        - jnp.mean(gain_applied, axis=-1, keepdims=True)
        - standardized_input * jnp.mean(gain_applied * standardized_input, axis=-1, keepdims=True)
    )
    grad_t = to_tiles(convolution_gradient)
    kernel_rows = []
    for r in range(kernel_size):
        row_terms = []
        for s in range(kernel_size):
            term = jnp.sum(
                grad_t * padded[r : r + tile_rows, s : s + tile_cols].astype(jnp.float32),
                axis=(0, 1),
            )
            row_terms.append(term.reshape(images, channel_total).sum(axis=0))
        kernel_rows.append(jnp.stack(row_terms))
    grad_kernel = jnp.stack(kernel_rows).reshape(kernel_size * kernel_size * channel_total)
    col_order = tuple(range(col_bits))
    row_order = (0, 1, 3, 2, 4)[:row_bits]
    pieces = 1 << (col_bits + row_bits)
    grad_kernel = grad_kernel.reshape(pieces, -1)
    grad_kernel = scatter_rows(grad_kernel, "cols", col_order)
    grad_kernel = scatter_rows(grad_kernel, "rows", row_order)
    grad_kernel = gather_rows(grad_kernel, "rows", row_order[::-1])
    grad_kernel = gather_rows(grad_kernel, "cols", col_order[::-1])
    grad_kernel = grad_kernel.reshape(kernel_size, kernel_size, channel_total) * scale
    grad_pad = with_halo(grad_t, (("rows", 0), ("cols", 1)), kernel_reach, jnp.bfloat16)
    total = to_tiles(out_grad).astype(jnp.float32)
    for r in range(kernel_size):
        for s in range(kernel_size):
            row_from = 2 * kernel_reach - r
            col_from = 2 * kernel_reach - s
            total = (
                total
                + taps[r, s]
                * grad_pad[row_from : row_from + tile_rows, col_from : col_from + tile_cols]
            )
    total = from_tiles(total)
    input_grad = total.astype(jnp.bfloat16)
    return (input_grad, grad_w1, grad_w2, grad_kernel)


def solution(mesh):
    return jax.shard_map(
        local,
        mesh=mesh,
        in_specs=(
            P(None, "rows", "cols", None),
            P(None, ("rows", "cols"), None),
            P(),
            P(),
            P("rows", "cols"),
            P("cols", "rows"),
            P(),
        ),
        out_specs=(P(None, "rows", "cols", None), P("rows", "cols"), P("cols", "rows"), P()),
        check_vma=False,
    )
```

```python
import jax
import jax.numpy as jnp
from jax import lax
from jax.sharding import PartitionSpec as P


def with_halo(value, sides, width, link_dtype=None):
    link_dtype = link_dtype or value.dtype
    for axis, dim in sides:
        peers, length = (lax.axis_size(axis), value.shape[dim])
        up = [(i, (i + 1) % peers) for i in range(peers - 1)]
        down = [(j, i) for i, j in up]
        last = lax.slice_in_dim(value, length - width, length, axis=dim).astype(link_dtype)
        first = lax.slice_in_dim(value, 0, width, axis=dim).astype(link_dtype)
        before = lax.ppermute(last, axis, up).astype(value.dtype)
        after = lax.ppermute(first, axis, down).astype(value.dtype)
        value = jnp.concatenate([before, value, after], axis=dim)
    return value


def swap_with(value, axis, bit):
    peers = lax.axis_size(axis)
    return lax.ppermute(value, axis, [(i, i ^ (1 << bit)) for i in range(peers)])


def gather_rows(value, axis, order):
    me = lax.axis_index(axis)
    for bit in order:
        other = swap_with(value, axis, bit)
        b = (me >> bit) & 1
        both = jnp.concatenate([value, other, value], axis=0)
        value = lax.dynamic_slice_in_dim(both, b * value.shape[0], 2 * value.shape[0], axis=0)
    n = len(order)
    block = value.shape[0] >> n
    rest = value.shape[1:]
    value = value.reshape((2,) * n + (block,) + rest)
    perm = [n - 1 - order.index(k) for k in reversed(range(n))]
    value = value.transpose(perm + list(range(n, value.ndim)))
    return value.reshape((block << n,) + rest)


def scatter_rows(value, axis, order, narrow_steps=0):
    me = lax.axis_index(axis)
    n = len(order)
    block = value.shape[0] >> n
    rest = value.shape[1:]
    value = value.reshape((2,) * n + (block,) + rest)
    perm = [n - 1 - order[j] for j in range(n)]
    value = value.transpose(perm + list(range(n, value.ndim))).reshape((block << n,) + rest)
    for step, bit in enumerate(order):
        half = value.shape[0] // 2
        b = (me >> bit) & 1
        keep = lax.dynamic_slice_in_dim(value, b * half, half, axis=0)
        send = lax.dynamic_slice_in_dim(value, (1 - b) * half, half, axis=0)
        if step < narrow_steps:
            got = swap_with(send.astype(jnp.bfloat16), axis, bit).astype(value.dtype)
        else:
            got = swap_with(send, axis, bit)
        value = keep + got
    return value


GATHER_ORDERS = ((4, 2, 3, 1, 0), (2, 4, 0, 3, 1), (4, 2, 1, 0, 3))
SCATTER_ORDERS = ((0, 1, 3, 2, 4), (1, 3, 0, 4, 2), (3, 0, 1, 2, 4))


def scatter_split(value):
    third = value.shape[1] // 3
    return jnp.concatenate(
        [
            scatter_rows(value[:, i * third : (i + 1) * third], "rows", order, 3)
            for i, order in enumerate(SCATTER_ORDERS)
        ],
        axis=1,
    )


def local(block_input, token_grads, conv_kernel, layer_norm_gain, w_in, w_out, layer_scale):
    images, tile_rows, tile_cols, channel_total = block_input.shape
    kernel_size = conv_kernel.shape[0]
    kernel_reach = kernel_size // 2
    n_rows = lax.axis_size("rows")
    n_cols = lax.axis_size("cols")
    row_bits = n_rows.bit_length() - 1
    col_bits = n_cols.bit_length() - 1
    run_count = tile_rows // 2
    half_cols = tile_cols // 2
    col_index = lax.axis_index("cols")

    hidden_cols = w_in.shape[1]
    both_weights = jnp.concatenate([w_in, w_out.T], axis=1)
    third = both_weights.shape[1] // 3
    gathered = jnp.concatenate(
        [
            gather_rows(both_weights[:, i * third : (i + 1) * third], "rows", order)
            for i, order in enumerate(GATHER_ORDERS)
        ],
        axis=1,
    )
    w_in_cols = gathered[:, :hidden_cols]
    w_out_cols_t = gathered[:, hidden_cols:]

    tokens = token_grads.reshape(images, 2, half_cols, 4 * channel_total)
    first_half = col_index // 2
    send_a = lax.dynamic_index_in_dim(tokens, first_half, 1, keepdims=False)
    send_b = lax.dynamic_index_in_dim(tokens, 1 - first_half, 1, keepdims=False)
    got_a = lax.ppermute(send_a, "cols", [(s, 2 * (s % 2) + s // 2) for s in range(n_cols)])
    got_b = lax.ppermute(send_b, "cols", [(s, 2 * (s % 2) + 1 - s // 2) for s in range(n_cols)])
    merged = lax.dynamic_slice_in_dim(
        jnp.stack([got_a, got_b, got_a], axis=1), col_index % 2, 2, axis=1
    )
    out_grad = merged.reshape(images, run_count, half_cols, 2, 2, channel_total)
    out_grad = out_grad.transpose(0, 1, 3, 2, 4, 5).reshape(
        images, tile_rows, tile_cols, channel_total
    )
    pixel_total = images * tile_rows * tile_cols
    branch_grad = (
        (out_grad.astype(jnp.float32) * layer_scale)
        .astype(jnp.bfloat16)
        .reshape(pixel_total, channel_total)
    )
    lane = 128
    groups = channel_total // lane

    def to_tiles(x):
        x = x.reshape(images, tile_rows, tile_cols, groups, lane).transpose(1, 2, 0, 3, 4)
        return x.reshape(tile_rows, tile_cols, images * groups, lane)

    def from_tiles(t):
        t = t.reshape(tile_rows, tile_cols, images, groups, lane).transpose(2, 0, 1, 3, 4)
        return t.reshape(images, tile_rows, tile_cols, channel_total)

    taps = jnp.tile(
        conv_kernel.reshape(kernel_size, kernel_size, 1, groups, lane), (1, 1, images, 1, 1)
    ).reshape(kernel_size, kernel_size, images * groups, lane)
    padded = with_halo(to_tiles(block_input), (("rows", 0), ("cols", 1)), kernel_reach)
    branch_all = lax.all_gather(branch_grad, "cols", axis=0, tiled=True)
    w_in_cols, w_out_cols_t, branch_all, padded = lax.optimization_barrier(
        (w_in_cols, w_out_cols_t, branch_all, padded)
    )
    conv_t = jnp.zeros((tile_rows, tile_cols, images * groups, lane), jnp.float32)
    for r in range(kernel_size):
        for s in range(kernel_size):
            conv_t = conv_t + taps[r, s] * padded[r : r + tile_rows, s : s + tile_cols].astype(
                jnp.float32
            )
    conv_out = from_tiles(conv_t)
    mean_val = jnp.mean(conv_out, axis=-1, keepdims=True)
    centered_input = conv_out - mean_val
    var_val = jnp.mean(centered_input * centered_input, axis=-1, keepdims=True)
    inverse_deviation = lax.rsqrt(var_val + 1e-06)
    standardized_input = centered_input * inverse_deviation
    norm_output = (
        (standardized_input * layer_norm_gain)
        .astype(jnp.bfloat16)
        .reshape(pixel_total, channel_total)
    )
    normed_all = lax.all_gather(norm_output, "cols", axis=0, tiled=True)
    pre = jnp.dot(normed_all, w_in_cols, preferred_element_type=jnp.float32)
    cdf = 0.5 * (1.0 + lax.erf(pre * 0.7071067811865476))
    hidden = (pre * cdf).astype(jnp.bfloat16)
    back_hidden = jnp.dot(branch_all, w_out_cols_t, preferred_element_type=jnp.float32)
    density = jnp.exp(-0.5 * pre * pre) * 0.3989422804014327
    hidden_grad = (back_hidden * (cdf + pre * density)).astype(jnp.bfloat16)
    scale = 1.0 / float(images * tile_rows * tile_cols * n_rows * n_cols) ** 0.5
    out_terms_t = lax.dot_general(
        branch_all, hidden, (((0,), (0,)), ((), ())), preferred_element_type=jnp.float32
    )
    in_terms = lax.dot_general(
        normed_all, hidden_grad, (((0,), (0,)), ((), ())), preferred_element_type=jnp.float32
    )
    grad_w2 = (scatter_split(out_terms_t) * scale).T
    grad_w1 = scatter_split(in_terms) * scale
    normed_grad = scatter_rows(
        lax.dot_general(
            hidden_grad, w_in_cols, (((1,), (1,)), ((), ())), preferred_element_type=jnp.float32
        ),
        "cols",
        (0, 1)[:col_bits],
        col_bits,
    )
    gain_applied = (
        normed_grad.reshape(images, tile_rows, tile_cols, channel_total) * layer_norm_gain
    )
    convolution_gradient = inverse_deviation * (
        gain_applied
        - jnp.mean(gain_applied, axis=-1, keepdims=True)
        - standardized_input * jnp.mean(gain_applied * standardized_input, axis=-1, keepdims=True)
    )
    grad_t = to_tiles(convolution_gradient)
    kernel_rows = []
    for r in range(kernel_size):
        row_terms = []
        for s in range(kernel_size):
            term = jnp.sum(
                grad_t * padded[r : r + tile_rows, s : s + tile_cols].astype(jnp.float32),
                axis=(0, 1),
            )
            row_terms.append(term.reshape(images, channel_total).sum(axis=0))
        kernel_rows.append(jnp.stack(row_terms))
    grad_kernel = jnp.stack(kernel_rows).reshape(kernel_size * kernel_size * channel_total)
    col_order = tuple(range(col_bits))
    row_order = (0, 1, 3, 2, 4)[:row_bits]
    pieces = 1 << (col_bits + row_bits)
    grad_kernel = grad_kernel.reshape(pieces, -1)
    grad_kernel = scatter_rows(grad_kernel, "cols", col_order)
    grad_kernel = scatter_rows(grad_kernel, "rows", row_order)
    grad_kernel = gather_rows(grad_kernel, "rows", row_order[::-1])
    grad_kernel = gather_rows(grad_kernel, "cols", col_order[::-1])
    grad_kernel = grad_kernel.reshape(kernel_size, kernel_size, channel_total) * scale
    grad_pad = with_halo(grad_t, (("rows", 0), ("cols", 1)), kernel_reach, jnp.bfloat16)
    total = to_tiles(out_grad).astype(jnp.float32)
    for r in range(kernel_size):
        for s in range(kernel_size):
            row_from = 2 * kernel_reach - r
            col_from = 2 * kernel_reach - s
            total = (
                total
                + taps[r, s]
                * grad_pad[row_from : row_from + tile_rows, col_from : col_from + tile_cols]
            )
    total = from_tiles(total)
    input_grad = total.astype(jnp.bfloat16)
    return (input_grad, grad_w1, grad_w2, grad_kernel)


def solution(mesh):
    return jax.shard_map(
        local,
        mesh=mesh,
        in_specs=(
            P(None, "rows", "cols", None),
            P(None, ("rows", "cols"), None),
            P(),
            P(),
            P("rows", "cols"),
            P("cols", "rows"),
            P(),
        ),
        out_specs=(P(None, "rows", "cols", None), P("rows", "cols"), P("cols", "rows"), P()),
        check_vma=False,
    )
```
